256 devices in a mesh: req: 32 (over x, z), tp: 8 (over y, core).
Axes of the slice: x: 4, y: 4, z: 8, core: 2. Of those that a mesh axis runs over, the one named last changes fastest.
Arguments:
- hidden: bfloat16 [4096, 2048], P('req', 'tp'), may hold values from -3 to 3
- lengths: int32 [4096], P('req'), may hold values from 1 to 1921, as said below
- routes: int32 [4096, 6], P('req'), may hold values from 0 to 63, all different within a row; in each aligned block of 128 rows (0 to 127, 128 to 255, ...) at most 32 rows name the same one
- latent_cache: bfloat16 [65536, 576], P('req'), may hold values from -400 to 400
- attention_gain: bfloat16 [2048], replicated, may hold values from 0.099609375 to 1.8984375
- query_weight: bfloat16 [2048, 3072], P(None, 'tp'), may hold values from -0.125 to 0.125
- latent_weight: bfloat16 [2048, 576], P(None, 'tp'), may hold values from -0.125 to 0.125
- latent_gain: bfloat16 [512], replicated, may hold values from 0.099609375 to 1.8984375
- key_absorb: bfloat16 [16, 128, 512], P('tp'), may hold values from -0.5 to 0.5
- value_absorb: bfloat16 [16, 512, 128], P('tp'), may hold values from -0.5 to 0.5
- output_weight: bfloat16 [2048, 2048], P('tp'), may hold values from -0.75 to 0.75
- feedforward_gain: bfloat16 [2048], replicated, may hold values from 0.099609375 to 1.8984375
- router_weight: bfloat16 [2048, 64], replicated, may hold values from -0.0625 to 0.0625
- expert_gate: bfloat16 [64, 2048, 1408], P('req', None, 'tp'), may hold values from -0.25 to 0.25
- expert_up: bfloat16 [64, 2048, 1408], P('req', None, 'tp'), may hold values from -0.25 to 0.25
- expert_down: bfloat16 [64, 1408, 2048], P('req', 'tp'), may hold values from -0.4375 to 0.4375
- shared_gate: bfloat16 [2048, 1408], P(None, 'tp'), may hold values from -0.25 to 0.25
- shared_up: bfloat16 [2048, 1408], P(None, 'tp'), may hold values from -0.25 to 0.25
- shared_down: bfloat16 [1408, 2048], P('tp'), may hold values from -0.21875 to 0.21875
Outputs:
- next_hidden: bfloat16 [4096, 2048], P('req', 'tp')
- new_rows: bfloat16 [4096, 576], P('req')
The draws below stay inside these ranges and needn't reach their ends.
Inputs may be any that keep to these rules, and one draw needn't show every extreme that they name: The lengths of the 128 requests of one index of req (aligned blocks of 128) sum to at most 2048, and to exactly 2048 on some index, where one request holds 1921. `routes`: among the rows of one index of req, no expert is named by more than 32 rows, a bound that some block reaches.
All inputs are finite; a program needn't handle non-finite values.
Results may differ from the reference program's by a relative error of at most 0.023.
The reference program's roundings to bfloat16 on the way count: a program that leaves them out, or rounds other values in their place, can miss the bound.
Values may be sent and summed in bfloat16 or wider, within the bound.
No kernel may reach another device: no remote copies, remote signals or barrier semaphores. Data moves between devices by JAX's collectives and lax.ppermute only.
A program may use at most 128 MiB of HBM per device.

```python
import math
import jax
import jax.numpy as jnp
import numpy as np
from jax import lax

D = 2048
HEADS = 16
NOPE = 128
ROPE = 64
LAT = 512
VHEAD = 128
FE = 1408
SH = 1408
TOPK = 6
R_DEV = 128
CAP_DEV = 2048
EXPERTS = 64
TOKENS = 4096
CACHE_ROWS = 65536
SLOTS = 32
N_REQ = 32


def draw_lengths(key, part):
    owners = TOKENS // R_DEV
    key_fill, key_top, key_weight = jax.random.split(jax.random.fold_in(key, 11), 3)
    fills = jax.random.randint(key_fill, (owners,), CAP_DEV // 4, CAP_DEV + 1)
    top_owner = jax.random.randint(key_top, (), 0, owners)
    base = jax.random.randint(key_weight, (owners, R_DEV), 1, 41)
    weights = base * base * base
    spare = fills - R_DEV
    shares = spare[:, None] * weights // jnp.sum(weights, axis=1, keepdims=True)
    result = 1 + shares
    leftover = fills - jnp.sum(result, axis=1)
    result = result.at[:, 0].add(leftover)
    longest = jnp.where(jnp.arange(R_DEV) == 0, CAP_DEV - R_DEV + 1, 1)
    result = jnp.where((jnp.arange(owners) == top_owner)[:, None], longest[None, :], result)
    return result.reshape(owners * R_DEV).astype(jnp.int32)


def draw_latent_cache(key, part):
    key_value = jax.random.fold_in(jax.random.fold_in(key, 23), 0)
    values = jax.random.normal(key_value, (CACHE_ROWS, LAT + ROPE), jnp.float32)
    values = jnp.clip(values, -6.0, 6.0)
    return values.astype(jnp.bfloat16)


def raised(drawn, rng, source, target, blocks, factor):
    owner, partner = [(jnp.arange(drawn.shape[axis_at]) // (drawn.shape[axis_at] // blocks)).reshape([-1 if axis == axis_at else 1 for axis in range(drawn.ndim)]) for axis_at in (source, target)]
    chosen = jax.random.permutation(rng, blocks)[partner]
    strong = (owner == chosen) | (owner == (partner + blocks // 2) % blocks)
    return jnp.where(strong, factor * drawn, drawn)


def shard_levels(key, shape, cuts, least, top_value):
    def one(axis_at, shards_of):
        draws = jax.random.uniform(jax.random.fold_in(jax.random.fold_in(key, 6), axis_at), (shards_of,), jnp.float32, least / len(cuts), top_value / len(cuts))
        return jnp.repeat(jnp.exp(draws), shape[axis_at] // shards_of).reshape((-1,) + (1,) * (len(shape) - axis_at - 1))

    gain = one(*cuts[0])
    for cut in cuts[1:]:
        gain = gain * one(*cut)
    return gain


def deal_out(key, own, number, rows, number_of, top, bound, lean):
    order = jax.random.permutation(key, number_of)
    heavy_load, common = load_shares(number_of, rows * top, bound, lean, True), load_shares(number_of, rows * top, bound, lean, False)
    places = jnp.arange(number_of)

    def named(tallies, rotation):
        used = int((tallies > 0).sum())
        fixed = max(1, used // 4)
        shifted = fixed + (places - fixed + rotation * (used - fixed)) % max(1, number_of - fixed)
        return jnp.zeros((number_of,), jnp.int32).at[order[jnp.where(places < fixed, places, shifted)]].set(jnp.asarray(tallies, jnp.int32))

    tallies = jnp.where(number % 4 == 0, named(heavy_load, number // 4), named(common, number - number // 4 - 1))
    mixed = jax.random.permutation(jax.random.fold_in(own, 3), number_of)
    giver, taker = mixed[0:number_of // 2 * 2:2], mixed[1:number_of // 2 * 2:2]
    slack = jnp.minimum(tallies[giver] - 1, bound - tallies[taker]) // 2
    slack = jnp.where((giver == order[0]) | (taker == order[0]) | (tallies[taker] == 0), 0, jnp.maximum(slack, 0))
    shifted = jax.random.randint(jax.random.fold_in(own, 4), (number_of // 2,), 0, 1 << 20) % (slack + 1)
    tallies = tallies.at[giver].add(-shifted).at[taker].add(shifted)
    members = jnp.searchsorted(jnp.cumsum(tallies), jnp.arange(rows * top), side="right").astype(jnp.int32)
    table = members.reshape(top, rows).T
    table = table[jax.random.permutation(jax.random.fold_in(own, 1), rows)]
    rotation = jax.random.randint(jax.random.fold_in(own, 2), (rows, 1), 0, top)
    return jnp.take_along_axis(table, (jnp.arange(top)[None, :] + rotation) % top, axis=1)


def load_shares(count, total, reach, slope, full):
    weights = [(1 << 20) // math.isqrt(standing ** slope) + 1 for standing in range(1, count + 1)]
    largest = reach if full else min(reach, max(-(-total // count), total * weights[0] // sum(weights)))
    least = 1 if total - largest >= count - 1 else 0
    counts, spare = [largest] + [least] * (count - 1), total - largest - least * (count - 1)
    while spare > 0:
        movable = [i for i in range(1, count) if counts[i] < largest] or [i for i in range(1, count) if counts[i] < reach]
        whole, budget = sum([weights[i] for i in movable]), spare
        for i in movable:
            addition = min(reach - counts[i], max(1, budget * weights[i] // whole), spare)
            counts[i] = counts[i] + addition
            spare = spare - addition
    return np.array(counts)


def scatter_about(own_key, shape, width, limit, cuts=(), kind=jnp.bfloat16):
    gain = shard_levels(own_key, shape, cuts, -0.22, 0.18) if cuts else 1.0
    values = jax.random.normal(own_key, shape, jnp.float32) * width * gain
    return jnp.minimum(jnp.maximum(values, -limit), limit).astype(kind)


def gaussian_with(own_key, dims, deviation, limit, cuts, heavy, held_as=jnp.bfloat16):
    values = deviation * jax.random.normal(own_key, dims, jnp.float32)
    if cuts:
        values = values * shard_levels(own_key, dims, cuts, -0.22, 0.18)
    return jnp.clip(raised(values, jax.random.fold_in(own_key, 3), *heavy), -limit, limit).astype(held_as)


def setup_inputs(seed: int = 0) -> dict:
    seeds = jax.random.split(jax.random.key(seed), 20)
    hidden = scatter_about(seeds[0], (TOKENS, D), 0.5, 3.0, ((0, 32), (1, 8)))
    lengths = draw_lengths(jax.random.fold_in(seeds[19], 71), 0)
    routes_keys = jax.random.split(jax.random.fold_in(seeds[2], 1), TOKENS // R_DEV)
    routes_turns = jax.random.permutation(jax.random.fold_in(seeds[2], 3), TOKENS // R_DEV)
    routes = jax.vmap(lambda own, number: deal_out(jax.random.fold_in(seeds[2], 2), own, number, R_DEV, EXPERTS, TOPK, SLOTS, 2))(routes_keys, routes_turns).reshape((TOKENS, TOPK))
    latent_cache = draw_latent_cache(jax.random.fold_in(seeds[19], 71), 0)
    attention_gain = jnp.clip(1.0 + 0.18 * jax.random.normal(seeds[4], (D,), jnp.float32), 0.099609375, 1.8984375).astype(jnp.bfloat16)
    query_weight = scatter_about(seeds[5], (D, HEADS * (NOPE + ROPE)), D ** -0.5, 0.125, ((1, 8),))
    latent_weight = scatter_about(seeds[6], (D, LAT + ROPE), D ** -0.5, 0.125, ((1, 8),))
    latent_gain = jnp.clip(1.0 + 0.18 * jax.random.normal(seeds[7], (LAT,), jnp.float32), 0.099609375, 1.8984375).astype(jnp.bfloat16)
    key_absorb = scatter_about(seeds[8], (HEADS, NOPE, LAT), NOPE ** -0.5, 0.5, ((0, 8),))
    value_absorb = scatter_about(seeds[9], (HEADS, LAT, VHEAD), (LAT // 4) ** -0.5, 0.5, ((0, 8),))
    output_weight = gaussian_with(seeds[10], (HEADS * VHEAD, D), (HEADS * VHEAD // 16) ** -0.5, 0.75, ((0, 8),), (0, 1, 8, 2.0))
    feedforward_gain = jnp.clip(1.0 + 0.18 * jax.random.normal(seeds[11], (D,), jnp.float32), 0.099609375, 1.8984375).astype(jnp.bfloat16)
    router_weight = scatter_about(seeds[12], (D, EXPERTS), (D * 5) ** -0.5, 0.0625)
    expert_gate = scatter_about(seeds[13], (EXPERTS, D, FE), (D // 4) ** -0.5, 0.25, ((0, 32), (2, 8)))
    expert_up = scatter_about(seeds[14], (EXPERTS, D, FE), (D // 4) ** -0.5, 0.25, ((0, 32), (2, 8)))
    expert_down = gaussian_with(seeds[15], (EXPERTS, FE, D), (FE // 4) ** -0.5, 0.4375, ((0, 32), (1, 8)), (1, 2, 8, 2.0))
    shared_gate = scatter_about(seeds[16], (D, SH), (D // 4) ** -0.5, 0.25, ((1, 8),))
    shared_up = scatter_about(seeds[17], (D, SH), (D // 4) ** -0.5, 0.25, ((1, 8),))
    shared_down = gaussian_with(seeds[18], (SH, D), SH ** -0.5, 0.21875, ((0, 8),), (0, 1, 8, 2.0))
    return {"hidden": hidden, "lengths": lengths, "routes": routes, "latent_cache": latent_cache, "attention_gain": attention_gain, "query_weight": query_weight, "latent_weight": latent_weight, "latent_gain": latent_gain, "key_absorb": key_absorb, "value_absorb": value_absorb, "output_weight": output_weight, "feedforward_gain": feedforward_gain, "router_weight": router_weight, "expert_gate": expert_gate, "expert_up": expert_up, "expert_down": expert_down, "shared_gate": shared_gate, "shared_up": shared_up, "shared_down": shared_down}


rope_base = 50000.0
route_scale = 2.446
norm_eps = 1e-06

def rms_norm(values, gains):
    widened = values.astype(jnp.float32)
    factor = lax.rsqrt(lax.optimization_barrier(jnp.mean(widened * widened, axis=-1, keepdims=True)) + norm_eps)
    return widened * factor * gains.astype(jnp.float32)

def rotate(values, positions):
    half_width = values.shape[-1] // 2
    exponent = jnp.arange(half_width, dtype=jnp.float32) * (2.0 / values.shape[-1])
    angles = positions[..., None] * jnp.power(rope_base, -exponent)
    cosine = jnp.cos(angles)
    sine_part = jnp.sin(angles)
    first_half = values[..., :half_width]
    second_half = values[..., half_width:]
    return jnp.concatenate([first_half * cosine - second_half * sine_part, first_half * sine_part + second_half * cosine], axis=-1)

def attend(queries, cache_rows, lengths, new_rows, score_scale, latent_width):
    starts = (jnp.cumsum(lengths) - lengths).astype(jnp.int32)
    places = jnp.arange(cache_rows.shape[0], dtype=jnp.int32)
    inside = (places[None, :] >= starts[:, None]) & (places[None, :] < (starts + lengths)[:, None])
    scores = jnp.einsum('rhk,jk->rhj', queries.astype(jnp.float32), cache_rows.astype(jnp.float32)) * score_scale
    own_score = lax.optimization_barrier(jnp.sum(queries.astype(jnp.float32) * new_rows.astype(jnp.float32)[:, None, :], axis=-1)) * score_scale
    highest = jnp.maximum(lax.optimization_barrier(jnp.max(jnp.where(inside[:, None, :], scores, -jnp.inf), axis=-1)), own_score)
    weights = jnp.where(inside[:, None, :], jnp.exp(scores - highest[..., None]), 0.0)
    own_weight = jnp.exp(own_score - highest)
    totals = lax.optimization_barrier(jnp.sum(weights, axis=-1)) + own_weight
    probabilities = (weights / totals[..., None]).astype(jnp.bfloat16)
    own_prob = (own_weight / totals).astype(jnp.bfloat16)
    summed = jnp.einsum('rhj,jl->rhl', probabilities.astype(jnp.float32), cache_rows[:, :latent_width].astype(jnp.float32))
    summed = summed + own_prob.astype(jnp.float32)[..., None] * new_rows[:, None, :latent_width].astype(jnp.float32)
    return summed.astype(jnp.bfloat16)

def reference(hidden, lengths, routes, latent_cache, attention_gain, query_weight, latent_weight, latent_gain, key_absorb, value_absorb, output_weight, feedforward_gain, router_weight, expert_gate, expert_up, expert_down, shared_gate, shared_up, shared_down):
    normed = rms_norm(hidden, attention_gain).astype(jnp.bfloat16)
    projected = jnp.dot(normed, query_weight, preferred_element_type=jnp.float32).reshape(TOKENS, HEADS, NOPE + ROPE)
    positions = lengths.astype(jnp.float32)
    query_nope = projected[..., :NOPE].astype(jnp.bfloat16)
    query_rope = rotate(projected[..., NOPE:], positions[:, None]).astype(jnp.bfloat16)
    query_latent = jnp.einsum('thn,hnl->thl', query_nope.astype(jnp.float32), key_absorb.astype(jnp.float32)).astype(jnp.bfloat16)
    latent_raw = jnp.dot(normed, latent_weight, preferred_element_type=jnp.float32).astype(jnp.bfloat16)
    latent_new = rms_norm(latent_raw[:, :LAT], latent_gain)
    key_new = rotate(latent_raw[:, LAT:].astype(jnp.float32), positions)
    new_rows = jnp.concatenate([latent_new, key_new], axis=-1).astype(jnp.bfloat16)
    queries = jnp.concatenate([query_latent, query_rope], axis=-1)
    score_scale = (NOPE + ROPE) ** (-0.5)

    def per_group(pieces):
        group_queries, group_cache, group_lengths, group_rows = pieces
        return attend(group_queries, group_cache, group_lengths, group_rows, score_scale, LAT)
    attended = lax.map(per_group, (queries.reshape(N_REQ, R_DEV, HEADS, LAT + ROPE), latent_cache.reshape(N_REQ, CAP_DEV, LAT + ROPE), lengths.reshape(N_REQ, R_DEV), new_rows.reshape(N_REQ, R_DEV, LAT + ROPE)))
    attended = attended.reshape(TOKENS, HEADS, LAT)
    head_values = jnp.einsum('thl,hlv->thv', attended.astype(jnp.float32), value_absorb.astype(jnp.float32)).astype(jnp.bfloat16)
    attention = jnp.dot(head_values.reshape(TOKENS, HEADS * VHEAD), output_weight, preferred_element_type=jnp.float32)
    mixed = (hidden.astype(jnp.float32) + attention).astype(jnp.bfloat16)
    expert_in = rms_norm(mixed, feedforward_gain).astype(jnp.bfloat16)
    logits = jnp.dot(expert_in, router_weight, preferred_element_type=jnp.float32)
    chosen = jnp.take_along_axis(jax.nn.sigmoid(logits), routes, axis=1)
    route_weights = chosen / lax.optimization_barrier(jnp.sum(chosen, axis=1, keepdims=True)) * route_scale
    expert_ids = routes.reshape(-1).astype(jnp.int32)
    flat_tokens = jnp.arange(TOKENS * TOPK, dtype=jnp.int32) // TOPK
    groups = flat_tokens // R_DEV
    onehot = (expert_ids[:, None] == jnp.arange(EXPERTS, dtype=jnp.int32)[None, :]).astype(jnp.int32)
    grouped = onehot.reshape(N_REQ, R_DEV * TOPK, EXPERTS)
    earlier = (jnp.cumsum(grouped, axis=1) - grouped).reshape(TOKENS * TOPK, EXPERTS)
    slot_index = lax.optimization_barrier(jnp.sum(earlier * onehot, axis=1)).astype(jnp.int32)
    column = (groups * SLOTS + slot_index).astype(jnp.int32)
    slot_tokens = jnp.zeros((EXPERTS, N_REQ * SLOTS), jnp.int32).at[expert_ids, column].set(flat_tokens)

    def per_expert(pieces):
        token_rows, gate_matrix, up_matrix, down_matrix = pieces
        taken_rows = expert_in[token_rows]
        gate_part = jnp.dot(taken_rows, gate_matrix, preferred_element_type=jnp.float32)
        up_part = jnp.dot(taken_rows, up_matrix, preferred_element_type=jnp.float32)
        inner_units = (jax.nn.silu(gate_part) * up_part).astype(jnp.bfloat16)
        return jnp.dot(inner_units, down_matrix, preferred_element_type=jnp.float32)
    expert_outs = lax.map(per_expert, (slot_tokens, expert_gate, expert_up, expert_down))
    picked = expert_outs[expert_ids, column].reshape(TOKENS, TOPK, D)
    routed = lax.optimization_barrier(jnp.sum(route_weights[..., None] * picked, axis=1))
    shared_inner = (jax.nn.silu(jnp.dot(expert_in, shared_gate, preferred_element_type=jnp.float32)) * jnp.dot(expert_in, shared_up, preferred_element_type=jnp.float32)).astype(jnp.bfloat16)
    shared = jnp.dot(shared_inner, shared_down, preferred_element_type=jnp.float32)
    next_hidden = (mixed.astype(jnp.float32) + routed + shared).astype(jnp.bfloat16)
    return (next_hidden, new_rows)
```

```python
import jax
import jax.numpy as jnp
from jax import lax
from jax.sharding import PartitionSpec as P

rope_base = 50000.0
route_scale = 2.446
norm_eps = 1e-06


def rms_norm(values, gains):
    widened = values.astype(jnp.float32)
    factor = lax.rsqrt(jnp.mean(widened * widened, axis=-1, keepdims=True) + norm_eps)
    return widened * factor * gains.astype(jnp.float32)


def rotate(values, positions):
    half_width = values.shape[-1] // 2
    exponent = jnp.arange(half_width, dtype=jnp.float32) * (2.0 / values.shape[-1])
    angles = positions[..., None] * jnp.power(rope_base, -exponent)
    cosine = jnp.cos(angles)
    sine_part = jnp.sin(angles)
    first_half = values[..., :half_width]
    second_half = values[..., half_width:]
    return jnp.concatenate(
        [
            first_half * cosine - second_half * sine_part,
            first_half * sine_part + second_half * cosine,
        ],
        axis=-1,
    )


def attend(queries, cache_rows, lengths, new_rows, score_scale, latent_width):
    starts = jnp.cumsum(lengths) - lengths
    places = jnp.arange(cache_rows.shape[0], dtype=jnp.int32)
    inside = (places[None, :] >= starts[:, None]) & (places[None, :] < (starts + lengths)[:, None])
    scores = (
        jnp.einsum("rhk,jk->rhj", queries, cache_rows, preferred_element_type=jnp.float32)
        * score_scale
    )
    own_score = (
        jnp.einsum("rhk,rk->rh", queries, new_rows, preferred_element_type=jnp.float32)
        * score_scale
    )
    highest = jnp.maximum(
        jnp.max(jnp.where(inside[:, None, :], scores, -jnp.inf), axis=-1), own_score
    )
    weights = jnp.where(inside[:, None, :], jnp.exp(scores - highest[..., None]), 0.0)
    own_weight = jnp.exp(own_score - highest)
    totals = jnp.sum(weights, axis=-1) + own_weight
    probabilities = (weights / totals[..., None]).astype(jnp.bfloat16)
    own_prob = (own_weight / totals).astype(jnp.bfloat16)
    summed = jnp.einsum(
        "rhj,jl->rhl",
        probabilities,
        cache_rows[:, :latent_width],
        preferred_element_type=jnp.float32,
    )
    summed = summed + own_prob.astype(jnp.float32)[..., None] * new_rows[
        :, None, :latent_width
    ].astype(jnp.float32)
    return summed.astype(jnp.bfloat16)


def shards(
    hidden,
    lengths,
    routes,
    latent_cache,
    attention_gain,
    query_weight,
    latent_weight,
    latent_gain,
    key_absorb,
    value_absorb,
    output_weight,
    feedforward_gain,
    router_weight,
    expert_gate,
    expert_up,
    expert_down,
    shared_gate,
    shared_up,
    shared_down,
):
    token_count = hidden.shape[0]
    owner_count = lax.axis_size("req")
    column_width = hidden.shape[1]
    column_start = lax.axis_index("tp") * column_width
    heads_here = key_absorb.shape[0]
    nope_width = key_absorb.shape[1]
    latent_width = key_absorb.shape[2]
    whole = lax.all_gather(hidden, "tp", axis=1, tiled=True)
    normed = rms_norm(whole, attention_gain).astype(jnp.bfloat16)
    projected = jnp.dot(normed, query_weight, preferred_element_type=jnp.float32).reshape(
        token_count, heads_here, -1
    )
    rope_width = projected.shape[2] - nope_width
    positions = lengths.astype(jnp.float32)
    query_nope = projected[..., :nope_width].astype(jnp.bfloat16)
    query_rope = rotate(projected[..., nope_width:], positions[:, None]).astype(jnp.bfloat16)
    query_latent = jnp.einsum(
        "thn,hnl->thl", query_nope, key_absorb, preferred_element_type=jnp.float32
    ).astype(jnp.bfloat16)
    latent_part = jnp.dot(normed, latent_weight, preferred_element_type=jnp.float32).astype(
        jnp.bfloat16
    )
    latent_raw = lax.all_gather(latent_part, "tp", axis=1, tiled=True)
    latent_new = rms_norm(latent_raw[:, :latent_width], latent_gain)
    key_new = rotate(latent_raw[:, latent_width:].astype(jnp.float32), positions)
    new_rows = jnp.concatenate([latent_new, key_new], axis=-1).astype(jnp.bfloat16)
    queries = jnp.concatenate([query_latent, query_rope], axis=-1)
    attended = attend(
        queries, latent_cache, lengths, new_rows, (nope_width + rope_width) ** (-0.5), latent_width
    )
    head_values = jnp.einsum(
        "thl,hlv->thv", attended, value_absorb, preferred_element_type=jnp.float32
    ).astype(jnp.bfloat16)
    attention = jnp.dot(
        head_values.reshape(token_count, -1), output_weight, preferred_element_type=jnp.float32
    )
    attention_columns = lax.psum_scatter(attention, "tp", scatter_dimension=1, tiled=True)
    mixed_columns = (hidden.astype(jnp.float32) + attention_columns).astype(jnp.bfloat16)
    mixed = lax.all_gather(mixed_columns, "tp", axis=1, tiled=True)
    expert_in = rms_norm(mixed, feedforward_gain).astype(jnp.bfloat16)
    logits = jnp.dot(expert_in, router_weight, preferred_element_type=jnp.float32)
    expert_count = router_weight.shape[1]
    top_count = routes.shape[1]
    per_owner = expert_count // owner_count
    slot_count = max(2, 8 * token_count * top_count // (3 * expert_count))
    chosen = jnp.take_along_axis(jax.nn.sigmoid(logits), routes, axis=1)
    route_weights = chosen / jnp.sum(chosen, axis=1, keepdims=True) * route_scale
    expert_ids = routes.reshape(-1)
    onehot = (expert_ids[:, None] == jnp.arange(expert_count, dtype=jnp.int32)[None, :]).astype(
        jnp.int32
    )
    earlier = jnp.cumsum(onehot, axis=0) - onehot
    slot_index = jnp.sum(earlier * onehot, axis=1)
    slot_places = (expert_ids * slot_count + slot_index).reshape(token_count, top_count)
    slot_total = expert_count * slot_count
    placed = slot_places[None, :, :] == jnp.arange(slot_total, dtype=jnp.int32)[:, None, None]
    gather_matrix = jnp.any(placed, axis=2).astype(jnp.bfloat16)
    combine_matrix = jnp.sum(jnp.where(placed, route_weights[None, :, :], 0.0), axis=2).T
    expert_columns = lax.dynamic_slice_in_dim(expert_in, column_start, column_width, 1)
    outgoing = jnp.dot(gather_matrix, expert_columns, preferred_element_type=jnp.float32).astype(
        jnp.bfloat16
    )
    outgoing = outgoing.reshape(owner_count, per_owner, slot_count, column_width)
    slab_columns = lax.all_to_all(outgoing, "req", split_axis=0, concat_axis=0, tiled=True)
    slab = lax.all_gather(slab_columns, "tp", axis=0, tiled=False)
    tp_count = slab.shape[0]
    gate_blocks = expert_gate.reshape(per_owner, tp_count, column_width, -1)
    up_blocks = expert_up.reshape(per_owner, tp_count, column_width, -1)
    gate_part = jnp.einsum(
        "toesc,etcf->oesf", slab, gate_blocks, preferred_element_type=jnp.float32
    )
    up_part = jnp.einsum("toesc,etcf->oesf", slab, up_blocks, preferred_element_type=jnp.float32)
    inner_units = (jax.nn.silu(gate_part) * up_part).astype(jnp.bfloat16)
    partial_out = jnp.einsum(
        "oesf,efd->oesd", inner_units, expert_down, preferred_element_type=jnp.float32
    )
    results = lax.psum_scatter(partial_out, "tp", scatter_dimension=3, tiled=True)
    shared_inner = (
        jax.nn.silu(jnp.dot(expert_in, shared_gate, preferred_element_type=jnp.float32))
        * jnp.dot(expert_in, shared_up, preferred_element_type=jnp.float32)
    ).astype(jnp.bfloat16)
    shared_part = jnp.dot(shared_inner, shared_down, preferred_element_type=jnp.float32)
    returned = lax.all_to_all(results, "req", split_axis=0, concat_axis=0, tiled=True)
    routed = jnp.dot(
        combine_matrix, returned.reshape(slot_total, column_width), precision=lax.Precision.HIGHEST
    )
    shared_columns = lax.psum_scatter(shared_part, "tp", scatter_dimension=1, tiled=True)
    next_hidden = (mixed_columns.astype(jnp.float32) + routed + shared_columns).astype(jnp.bfloat16)
    return (next_hidden, new_rows)


def solution(mesh):
    in_specs = (
        P("req", "tp"),
        P("req"),
        P("req", None),
        P("req", None),
        P(),
        P(None, "tp"),
        P(None, "tp"),
        P(),
        P("tp", None, None),
        P("tp", None, None),
        P("tp", None),
        P(),
        P(),
        P("req", None, "tp"),
        P("req", None, "tp"),
        P("req", "tp", None),
        P(None, "tp"),
        P(None, "tp"),
        P("tp", None),
    )
    out_specs = (P("req", "tp"), P("req", None))
    return jax.shard_map(shards, mesh=mesh, in_specs=in_specs, out_specs=out_specs, check_vma=False)
```

```python
import jax
import jax.numpy as jnp
from jax import lax
from jax.sharding import PartitionSpec as P

rope_base = 50000.0
route_scale = 2.446
norm_eps = 1e-06


def rms_norm(values, gains):
    widened = values.astype(jnp.float32)
    factor = lax.rsqrt(jnp.mean(widened * widened, axis=-1, keepdims=True) + norm_eps)
    return widened * factor * gains.astype(jnp.float32)


def rotate(values, positions):
    half_width = values.shape[-1] // 2
    exponent = jnp.arange(half_width, dtype=jnp.float32) * (2.0 / values.shape[-1])
    angles = positions[..., None] * jnp.power(rope_base, -exponent)
    cosine = jnp.cos(angles)
    sine_part = jnp.sin(angles)
    first_half = values[..., :half_width]
    second_half = values[..., half_width:]
    return jnp.concatenate(
        [
            first_half * cosine - second_half * sine_part,
            first_half * sine_part + second_half * cosine,
        ],
        axis=-1,
    )


def attend(queries, cache_rows, lengths, new_rows, score_scale, latent_width):
    starts = jnp.cumsum(lengths) - lengths
    places = jnp.arange(cache_rows.shape[0], dtype=jnp.int32)
    inside = (places[None, :] >= starts[:, None]) & (places[None, :] < (starts + lengths)[:, None])
    scores = (
        jnp.einsum("rhk,jk->rhj", queries, cache_rows, preferred_element_type=jnp.float32)
        * score_scale
    )
    own_score = (
        jnp.einsum("rhk,rk->rh", queries, new_rows, preferred_element_type=jnp.float32)
        * score_scale
    )
    highest = jnp.maximum(
        jnp.max(jnp.where(inside[:, None, :], scores, -jnp.inf), axis=-1), own_score
    )
    weights = jnp.where(inside[:, None, :], jnp.exp(scores - highest[..., None]), 0.0)
    own_weight = jnp.exp(own_score - highest)
    totals = jnp.sum(weights, axis=-1) + own_weight
    probabilities = (weights / totals[..., None]).astype(jnp.bfloat16)
    own_prob = (own_weight / totals).astype(jnp.bfloat16)
    summed = jnp.einsum(
        "rhj,jl->rhl",
        probabilities,
        cache_rows[:, :latent_width],
        preferred_element_type=jnp.float32,
    )
    summed = summed + own_prob.astype(jnp.float32)[..., None] * new_rows[
        :, None, :latent_width
    ].astype(jnp.float32)
    return summed.astype(jnp.bfloat16)


def shards(
    hidden,
    lengths,
    routes,
    latent_cache,
    attention_gain,
    query_weight,
    latent_weight,
    latent_gain,
    key_absorb,
    value_absorb,
    output_weight,
    feedforward_gain,
    router_weight,
    expert_gate,
    expert_up,
    expert_down,
    shared_gate,
    shared_up,
    shared_down,
):
    token_count = hidden.shape[0]
    owner_count = lax.axis_size("req")
    column_width = hidden.shape[1]
    column_start = lax.axis_index("tp") * column_width
    heads_here = key_absorb.shape[0]
    nope_width = key_absorb.shape[1]
    latent_width = key_absorb.shape[2]
    whole = lax.all_gather(hidden, "tp", axis=1, tiled=True)
    normed = rms_norm(whole, attention_gain).astype(jnp.bfloat16)
    projected = jnp.dot(normed, query_weight, preferred_element_type=jnp.float32).reshape(
        token_count, heads_here, -1
    )
    rope_width = projected.shape[2] - nope_width
    positions = lengths.astype(jnp.float32)
    query_nope = projected[..., :nope_width].astype(jnp.bfloat16)
    query_rope = rotate(projected[..., nope_width:], positions[:, None]).astype(jnp.bfloat16)
    query_latent = jnp.einsum(
        "thn,hnl->thl", query_nope, key_absorb, preferred_element_type=jnp.float32
    ).astype(jnp.bfloat16)
    latent_part = jnp.dot(normed, latent_weight, preferred_element_type=jnp.float32).astype(
        jnp.bfloat16
    )
    latent_raw = lax.all_gather(latent_part, "tp", axis=1, tiled=True)
    latent_new = rms_norm(latent_raw[:, :latent_width], latent_gain)
    key_new = rotate(latent_raw[:, latent_width:].astype(jnp.float32), positions)
    new_rows = jnp.concatenate([latent_new, key_new], axis=-1).astype(jnp.bfloat16)
    queries = jnp.concatenate([query_latent, query_rope], axis=-1)
    attended = attend(
        queries, latent_cache, lengths, new_rows, (nope_width + rope_width) ** (-0.5), latent_width
    )
    head_values = jnp.einsum(
        "thl,hlv->thv", attended, value_absorb, preferred_element_type=jnp.float32
    ).astype(jnp.bfloat16)
    attention = jnp.dot(
        head_values.reshape(token_count, -1), output_weight, preferred_element_type=jnp.float32
    )
    attention_columns = lax.psum_scatter(attention, "tp", scatter_dimension=1, tiled=True)
    mixed_columns = (hidden.astype(jnp.float32) + attention_columns).astype(jnp.bfloat16)
    mixed = lax.all_gather(mixed_columns, "tp", axis=1, tiled=True)
    expert_in = rms_norm(mixed, feedforward_gain).astype(jnp.bfloat16)
    logits = jnp.dot(expert_in, router_weight, preferred_element_type=jnp.float32)
    expert_count = router_weight.shape[1]
    top_count = routes.shape[1]
    per_owner = expert_count // owner_count
    slot_count = max(2, 8 * token_count * top_count // (3 * expert_count))
    chosen = jnp.take_along_axis(jax.nn.sigmoid(logits), routes, axis=1)
    route_weights = chosen / jnp.sum(chosen, axis=1, keepdims=True) * route_scale
    expert_ids = routes.reshape(-1)
    onehot = (expert_ids[:, None] == jnp.arange(expert_count, dtype=jnp.int32)[None, :]).astype(
        jnp.int32
    )
    earlier = jnp.cumsum(onehot, axis=0) - onehot
    slot_index = jnp.sum(earlier * onehot, axis=1)
    slot_places = (expert_ids * slot_count + slot_index).reshape(token_count, top_count)
    slot_total = expert_count * slot_count
    placed = slot_places[None, :, :] == jnp.arange(slot_total, dtype=jnp.int32)[:, None, None]
    gather_matrix = jnp.any(placed, axis=2).astype(jnp.bfloat16)
    combine_matrix = jnp.sum(jnp.where(placed, route_weights[None, :, :], 0.0), axis=2).T
    expert_columns = lax.dynamic_slice_in_dim(expert_in, column_start, column_width, 1)
    outgoing = jnp.dot(gather_matrix, expert_columns, preferred_element_type=jnp.float32).astype(
        jnp.bfloat16
    )
    outgoing = outgoing.reshape(owner_count, per_owner, slot_count, column_width)
    slab_columns = lax.all_to_all(outgoing, "req", split_axis=0, concat_axis=0, tiled=True)
    slab = lax.all_gather(slab_columns, "tp", axis=0, tiled=False)
    tp_count = slab.shape[0]
    gate_blocks = expert_gate.reshape(per_owner, tp_count, column_width, -1)
    up_blocks = expert_up.reshape(per_owner, tp_count, column_width, -1)
    gate_part = jnp.einsum(
        "toesc,etcf->oesf", slab, gate_blocks, preferred_element_type=jnp.float32
    )
    up_part = jnp.einsum("toesc,etcf->oesf", slab, up_blocks, preferred_element_type=jnp.float32)
    inner_units = (jax.nn.silu(gate_part) * up_part).astype(jnp.bfloat16)
    partial_out = jnp.einsum(
        "oesf,efd->oesd", inner_units, expert_down, preferred_element_type=jnp.float32
    )
    shared_inner = (
        jax.nn.silu(jnp.dot(expert_in, shared_gate, preferred_element_type=jnp.float32))
        * jnp.dot(expert_in, shared_up, preferred_element_type=jnp.float32)
    ).astype(jnp.bfloat16)
    shared_part = jnp.dot(shared_inner, shared_down, preferred_element_type=jnp.float32)
    both_parts = jnp.concatenate(
        [partial_out.reshape(slot_total, -1), shared_part], axis=0
    ).astype(jnp.bfloat16)
    both_columns = lax.psum_scatter(both_parts, "tp", scatter_dimension=1, tiled=True)
    results = both_columns[:slot_total].reshape(owner_count, per_owner, slot_count, column_width)
    shared_columns = both_columns[slot_total:].astype(jnp.float32)
    returned = lax.all_to_all(results, "req", split_axis=0, concat_axis=0, tiled=True)
    routed = jnp.dot(
        combine_matrix,
        returned.reshape(slot_total, column_width).astype(jnp.float32),
        precision=lax.Precision.HIGHEST,
    )
    next_hidden = (mixed_columns.astype(jnp.float32) + routed + shared_columns).astype(jnp.bfloat16)
    return (next_hidden, new_rows)


def solution(mesh):
    in_specs = (
        P("req", "tp"),
        P("req"),
        P("req", None),
        P("req", None),
        P(),
        P(None, "tp"),
        P(None, "tp"),
        P(),
        P("tp", None, None),
        P("tp", None, None),
        P("tp", None),
        P(),
        P(),
        P("req", None, "tp"),
        P("req", None, "tp"),
        P("req", "tp", None),
        P(None, "tp"),
        P(None, "tp"),
        P("tp", None),
    )
    out_specs = (P("req", "tp"), P("req", None))
    return jax.shard_map(shards, mesh=mesh, in_specs=in_specs, out_specs=out_specs, check_vma=False)
```

```python
import jax
import jax.numpy as jnp
from jax import lax
from jax.sharding import PartitionSpec as P

rope_base = 50000.0
route_scale = 2.446
norm_eps = 1e-06


def rms_norm(values, gains):
    widened = values.astype(jnp.float32)
    factor = lax.rsqrt(jnp.mean(widened * widened, axis=-1, keepdims=True) + norm_eps)
    return widened * factor * gains.astype(jnp.float32)


def rotate(values, positions):
    half_width = values.shape[-1] // 2
    exponent = jnp.arange(half_width, dtype=jnp.float32) * (2.0 / values.shape[-1])
    angles = positions[..., None] * jnp.power(rope_base, -exponent)
    cosine = jnp.cos(angles)
    sine_part = jnp.sin(angles)
    first_half = values[..., :half_width]
    second_half = values[..., half_width:]
    return jnp.concatenate(
        [
            first_half * cosine - second_half * sine_part,
            first_half * sine_part + second_half * cosine,
        ],
        axis=-1,
    )


def attend(queries, cache_rows, lengths, new_rows, score_scale, latent_width):
    starts = jnp.cumsum(lengths) - lengths
    places = jnp.arange(cache_rows.shape[0], dtype=jnp.int32)
    inside = (places[None, :] >= starts[:, None]) & (places[None, :] < (starts + lengths)[:, None])
    scores = (
        jnp.einsum("rhk,jk->rhj", queries, cache_rows, preferred_element_type=jnp.float32)
        * score_scale
    )
    own_score = (
        jnp.einsum("rhk,rk->rh", queries, new_rows, preferred_element_type=jnp.float32)
        * score_scale
    )
    highest = jnp.maximum(
        jnp.max(jnp.where(inside[:, None, :], scores, -jnp.inf), axis=-1), own_score
    )
    weights = jnp.where(inside[:, None, :], jnp.exp(scores - highest[..., None]), 0.0)
    own_weight = jnp.exp(own_score - highest)
    totals = jnp.sum(weights, axis=-1) + own_weight
    probabilities = (weights / totals[..., None]).astype(jnp.bfloat16)
    own_prob = (own_weight / totals).astype(jnp.bfloat16)
    summed = jnp.einsum(
        "rhj,jl->rhl",
        probabilities,
        cache_rows[:, :latent_width],
        preferred_element_type=jnp.float32,
    )
    summed = summed + own_prob.astype(jnp.float32)[..., None] * new_rows[
        :, None, :latent_width
    ].astype(jnp.float32)
    return summed.astype(jnp.bfloat16)


def shards(
    hidden,
    lengths,
    routes,
    latent_cache,
    attention_gain,
    query_weight,
    latent_weight,
    latent_gain,
    key_absorb,
    value_absorb,
    output_weight,
    feedforward_gain,
    router_weight,
    expert_gate,
    expert_up,
    expert_down,
    shared_gate,
    shared_up,
    shared_down,
):
    token_count = hidden.shape[0]
    owner_count = lax.axis_size("req")
    column_width = hidden.shape[1]
    column_start = lax.axis_index("tp") * column_width
    heads_here = key_absorb.shape[0]
    nope_width = key_absorb.shape[1]
    latent_width = key_absorb.shape[2]
    whole = lax.all_gather(hidden, "tp", axis=1, tiled=True)
    normed = rms_norm(whole, attention_gain).astype(jnp.bfloat16)
    projected = jnp.dot(normed, query_weight, preferred_element_type=jnp.float32).reshape(
        token_count, heads_here, -1
    )
    rope_width = projected.shape[2] - nope_width
    positions = lengths.astype(jnp.float32)
    query_nope = projected[..., :nope_width].astype(jnp.bfloat16)
    query_rope = rotate(projected[..., nope_width:], positions[:, None]).astype(jnp.bfloat16)
    query_latent = jnp.einsum(
        "thn,hnl->thl", query_nope, key_absorb, preferred_element_type=jnp.float32
    ).astype(jnp.bfloat16)
    latent_part = jnp.dot(normed, latent_weight, preferred_element_type=jnp.float32).astype(
        jnp.bfloat16
    )
    latent_raw = lax.all_gather(latent_part, "tp", axis=1, tiled=True)
    latent_new = rms_norm(latent_raw[:, :latent_width], latent_gain)
    key_new = rotate(latent_raw[:, latent_width:].astype(jnp.float32), positions)
    new_rows = jnp.concatenate([latent_new, key_new], axis=-1).astype(jnp.bfloat16)
    queries = jnp.concatenate([query_latent, query_rope], axis=-1)
    attended = attend(
        queries, latent_cache, lengths, new_rows, (nope_width + rope_width) ** (-0.5), latent_width
    )
    head_values = jnp.einsum(
        "thl,hlv->thv", attended, value_absorb, preferred_element_type=jnp.float32
    ).astype(jnp.bfloat16)
    attention = jnp.dot(
        head_values.reshape(token_count, -1), output_weight, preferred_element_type=jnp.float32
    )
    tp_count = lax.axis_size("tp")
    attention_blocks = attention.reshape(token_count, tp_count, column_width).transpose(1, 0, 2)
    attention_blocks = lax.all_to_all(attention_blocks, "tp", split_axis=0, concat_axis=0, tiled=True)
    attention_columns = jnp.sum(attention_blocks, axis=0)
    mixed_columns = (hidden.astype(jnp.float32) + attention_columns).astype(jnp.bfloat16)
    mixed = lax.all_gather(mixed_columns, "tp", axis=1, tiled=True)
    expert_in = rms_norm(mixed, feedforward_gain).astype(jnp.bfloat16)
    logits = jnp.dot(expert_in, router_weight, preferred_element_type=jnp.float32)
    expert_count = router_weight.shape[1]
    top_count = routes.shape[1]
    per_owner = expert_count // owner_count
    slot_count = max(2, 8 * token_count * top_count // (3 * expert_count))
    chosen = jnp.take_along_axis(jax.nn.sigmoid(logits), routes, axis=1)
    route_weights = chosen / jnp.sum(chosen, axis=1, keepdims=True) * route_scale
    expert_ids = routes.reshape(-1)
    onehot = (expert_ids[:, None] == jnp.arange(expert_count, dtype=jnp.int32)[None, :]).astype(
        jnp.int32
    )
    earlier = jnp.cumsum(onehot, axis=0) - onehot
    slot_index = jnp.sum(earlier * onehot, axis=1)
    slot_places = (expert_ids * slot_count + slot_index).reshape(token_count, top_count)
    slot_total = expert_count * slot_count
    placed = slot_places[None, :, :] == jnp.arange(slot_total, dtype=jnp.int32)[:, None, None]
    gather_matrix = jnp.any(placed, axis=2).astype(jnp.bfloat16)
    combine_matrix = jnp.sum(jnp.where(placed, route_weights[None, :, :], 0.0), axis=2).T
    expert_columns = lax.dynamic_slice_in_dim(expert_in, column_start, column_width, 1)
    outgoing = jnp.dot(gather_matrix, expert_columns, preferred_element_type=jnp.float32).astype(
        jnp.bfloat16
    )
    outgoing = outgoing.reshape(owner_count, per_owner, slot_count, column_width)
    slab_columns = lax.all_to_all(outgoing, "req", split_axis=0, concat_axis=0, tiled=True)
    slab = lax.all_gather(slab_columns, "tp", axis=0, tiled=False)
    gate_blocks = expert_gate.reshape(per_owner, tp_count, column_width, -1)
    up_blocks = expert_up.reshape(per_owner, tp_count, column_width, -1)
    gate_part = jnp.einsum(
        "toesc,etcf->eosf", slab, gate_blocks, preferred_element_type=jnp.float32
    )
    up_part = jnp.einsum("toesc,etcf->eosf", slab, up_blocks, preferred_element_type=jnp.float32)
    inner_units = (jax.nn.silu(gate_part) * up_part).astype(jnp.bfloat16)
    partial_out = jnp.einsum(
        "eosf,efd->eosd", inner_units, expert_down, preferred_element_type=jnp.float32
    )
    shared_inner = (
        jax.nn.silu(jnp.dot(expert_in, shared_gate, preferred_element_type=jnp.float32))
        * jnp.dot(expert_in, shared_up, preferred_element_type=jnp.float32)
    ).astype(jnp.bfloat16)
    shared_part = jnp.dot(shared_inner, shared_down, preferred_element_type=jnp.float32)
    both_parts = jnp.concatenate(
        [partial_out.reshape(slot_total, -1), shared_part], axis=0
    ).astype(jnp.bfloat16)
    both_columns = lax.psum_scatter(both_parts, "tp", scatter_dimension=1, tiled=True)
    expert_sums = both_columns[:slot_total]
    shared_sums = both_columns[slot_total:]
    results = expert_sums.reshape(per_owner, owner_count, slot_count, column_width).transpose(
        1, 0, 2, 3
    )
    shared_columns = shared_sums.astype(jnp.float32)
    returned = lax.all_to_all(results, "req", split_axis=0, concat_axis=0, tiled=True)
    routed = jnp.dot(
        combine_matrix,
        returned.reshape(slot_total, column_width).astype(jnp.float32),
        precision=lax.Precision.HIGHEST,
    )
    next_hidden = (mixed_columns.astype(jnp.float32) + routed + shared_columns).astype(jnp.bfloat16)
    return (next_hidden, new_rows)


def solution(mesh):
    in_specs = (
        P("req", "tp"),
        P("req"),
        P("req", None),
        P("req", None),
        P(),
        P(None, "tp"),
        P(None, "tp"),
        P(),
        P("tp", None, None),
        P("tp", None, None),
        P("tp", None),
        P(),
        P(),
        P("req", None, "tp"),
        P("req", None, "tp"),
        P("req", "tp", None),
        P(None, "tp"),
        P(None, "tp"),
        P("tp", None),
    )
    out_specs = (P("req", "tp"), P("req", None))
    return jax.shard_map(shards, mesh=mesh, in_specs=in_specs, out_specs=out_specs, check_vma=False)
```

```python
import jax
import jax.numpy as jnp
from jax import lax
from jax.sharding import Mesh, PartitionSpec as P

rope_base = 50000.0
route_scale = 2.446
norm_eps = 1e-06


def rms_norm(values, gains):
    widened = values.astype(jnp.float32)
    factor = lax.rsqrt(jnp.mean(widened * widened, axis=-1, keepdims=True) + norm_eps)
    return widened * factor * gains.astype(jnp.float32)


def rotate(values, positions):
    half_width = values.shape[-1] // 2
    exponent = jnp.arange(half_width, dtype=jnp.float32) * (2.0 / values.shape[-1])
    angles = positions[..., None] * jnp.power(rope_base, -exponent)
    cosine = jnp.cos(angles)
    sine_part = jnp.sin(angles)
    first_half = values[..., :half_width]
    second_half = values[..., half_width:]
    return jnp.concatenate(
        [
            first_half * cosine - second_half * sine_part,
            first_half * sine_part + second_half * cosine,
        ],
        axis=-1,
    )


def attend(queries, cache_rows, lengths, new_rows, score_scale, latent_width):
    starts = jnp.cumsum(lengths) - lengths
    places = jnp.arange(cache_rows.shape[0], dtype=jnp.int32)
    inside = (places[None, :] >= starts[:, None]) & (places[None, :] < (starts + lengths)[:, None])
    scores = (
        jnp.einsum("rhk,jk->rhj", queries, cache_rows, preferred_element_type=jnp.float32)
        * score_scale
    )
    own_score = (
        jnp.einsum("rhk,rk->rh", queries, new_rows, preferred_element_type=jnp.float32)
        * score_scale
    )
    highest = jnp.maximum(
        jnp.max(jnp.where(inside[:, None, :], scores, -jnp.inf), axis=-1), own_score
    )
    weights = jnp.where(inside[:, None, :], jnp.exp(scores - highest[..., None]), 0.0)
    own_weight = jnp.exp(own_score - highest)
    totals = jnp.sum(weights, axis=-1) + own_weight
    probabilities = (weights / totals[..., None]).astype(jnp.bfloat16)
    own_prob = (own_weight / totals).astype(jnp.bfloat16)
    summed = jnp.einsum(
        "rhj,jl->rhl",
        probabilities,
        cache_rows[:, :latent_width],
        preferred_element_type=jnp.float32,
    )
    summed = summed + own_prob.astype(jnp.float32)[..., None] * new_rows[
        :, None, :latent_width
    ].astype(jnp.float32)
    return summed.astype(jnp.bfloat16)


REQ_AXES = ("req_hi", "req_lo")


def req_all_to_all(values):
    high = lax.axis_size(REQ_AXES[0])
    low = lax.axis_size(REQ_AXES[1])
    staged = values.reshape(high, low, *values.shape[1:])
    staged = lax.all_to_all(staged, REQ_AXES[1], split_axis=1, concat_axis=1, tiled=True)
    staged = lax.all_to_all(staged, REQ_AXES[0], split_axis=0, concat_axis=0, tiled=True)
    return staged.reshape(values.shape)


def split_mesh(mesh):
    column = mesh.devices[:, 0]
    low = len({device.coords[2] for device in column})
    if low < 1 or column.size % low:
        low = 1
    devices = mesh.devices.reshape(column.size // low, low, mesh.devices.shape[1])
    return Mesh(devices, REQ_AXES + ("tp",))


def shards(
    hidden,
    lengths,
    routes,
    latent_cache,
    attention_gain,
    query_weight,
    latent_weight,
    latent_gain,
    key_absorb,
    value_absorb,
    output_weight,
    feedforward_gain,
    router_weight,
    expert_gate,
    expert_up,
    expert_down,
    shared_gate,
    shared_up,
    shared_down,
):
    token_count = hidden.shape[0]
    owner_count = lax.axis_size(REQ_AXES)
    column_width = hidden.shape[1]
    column_start = lax.axis_index("tp") * column_width
    heads_here = key_absorb.shape[0]
    nope_width = key_absorb.shape[1]
    latent_width = key_absorb.shape[2]
    whole = lax.all_gather(hidden, "tp", axis=1, tiled=True)
    normed = rms_norm(whole, attention_gain).astype(jnp.bfloat16)
    projected = jnp.dot(normed, query_weight, preferred_element_type=jnp.float32).reshape(
        token_count, heads_here, -1
    )
    rope_width = projected.shape[2] - nope_width
    positions = lengths.astype(jnp.float32)
    query_nope = projected[..., :nope_width].astype(jnp.bfloat16)
    query_rope = rotate(projected[..., nope_width:], positions[:, None]).astype(jnp.bfloat16)
    query_latent = jnp.einsum(
        "thn,hnl->thl", query_nope, key_absorb, preferred_element_type=jnp.float32
    ).astype(jnp.bfloat16)
    latent_part = jnp.dot(normed, latent_weight, preferred_element_type=jnp.float32).astype(
        jnp.bfloat16
    )
    latent_raw = lax.all_gather(latent_part, "tp", axis=1, tiled=True)
    latent_new = rms_norm(latent_raw[:, :latent_width], latent_gain)
    key_new = rotate(latent_raw[:, latent_width:].astype(jnp.float32), positions)
    new_rows = jnp.concatenate([latent_new, key_new], axis=-1).astype(jnp.bfloat16)
    queries = jnp.concatenate([query_latent, query_rope], axis=-1)
    attended = attend(
        queries, latent_cache, lengths, new_rows, (nope_width + rope_width) ** (-0.5), latent_width
    )
    head_values = jnp.einsum(
        "thl,hlv->thv", attended, value_absorb, preferred_element_type=jnp.float32
    ).astype(jnp.bfloat16)
    attention = jnp.dot(
        head_values.reshape(token_count, -1), output_weight, preferred_element_type=jnp.float32
    )
    tp_count = lax.axis_size("tp")
    attention_blocks = attention.reshape(token_count, tp_count, column_width).transpose(1, 0, 2)
    attention_blocks = lax.all_to_all(attention_blocks, "tp", split_axis=0, concat_axis=0, tiled=True)
    attention_columns = jnp.sum(attention_blocks, axis=0)
    mixed_columns = (hidden.astype(jnp.float32) + attention_columns).astype(jnp.bfloat16)
    mixed = lax.all_gather(mixed_columns, "tp", axis=1, tiled=True)
    expert_in = rms_norm(mixed, feedforward_gain).astype(jnp.bfloat16)
    logits = jnp.dot(expert_in, router_weight, preferred_element_type=jnp.float32)
    expert_count = router_weight.shape[1]
    top_count = routes.shape[1]
    per_owner = expert_count // owner_count
    slot_count = max(2, 8 * token_count * top_count // (3 * expert_count))
    chosen = jnp.take_along_axis(jax.nn.sigmoid(logits), routes, axis=1)
    route_weights = chosen / jnp.sum(chosen, axis=1, keepdims=True) * route_scale
    expert_ids = routes.reshape(-1)
    onehot = (expert_ids[:, None] == jnp.arange(expert_count, dtype=jnp.int32)[None, :]).astype(
        jnp.int32
    )
    earlier = jnp.cumsum(onehot, axis=0) - onehot
    slot_index = jnp.sum(earlier * onehot, axis=1)
    slot_places = (expert_ids * slot_count + slot_index).reshape(token_count, top_count)
    slot_total = expert_count * slot_count
    placed = slot_places[None, :, :] == jnp.arange(slot_total, dtype=jnp.int32)[:, None, None]
    gather_matrix = jnp.any(placed, axis=2).astype(jnp.bfloat16)
    combine_matrix = jnp.sum(jnp.where(placed, route_weights[None, :, :], 0.0), axis=2).T
    expert_columns = lax.dynamic_slice_in_dim(expert_in, column_start, column_width, 1)
    outgoing = jnp.dot(gather_matrix, expert_columns, preferred_element_type=jnp.float32).astype(
        jnp.bfloat16
    )
    outgoing = outgoing.reshape(owner_count, per_owner, slot_count, column_width)
    slab_columns = req_all_to_all(outgoing)
    slab = lax.all_gather(slab_columns, "tp", axis=0, tiled=False)
    gate_blocks = expert_gate.reshape(per_owner, tp_count, column_width, -1)
    up_blocks = expert_up.reshape(per_owner, tp_count, column_width, -1)
    gate_part = jnp.einsum(
        "toesc,etcf->eosf", slab, gate_blocks, preferred_element_type=jnp.float32
    )
    up_part = jnp.einsum("toesc,etcf->eosf", slab, up_blocks, preferred_element_type=jnp.float32)
    inner_units = (jax.nn.silu(gate_part) * up_part).astype(jnp.bfloat16)
    partial_out = jnp.einsum(
        "eosf,efd->eosd", inner_units, expert_down, preferred_element_type=jnp.float32
    )
    shared_inner = (
        jax.nn.silu(jnp.dot(expert_in, shared_gate, preferred_element_type=jnp.float32))
        * jnp.dot(expert_in, shared_up, preferred_element_type=jnp.float32)
    ).astype(jnp.bfloat16)
    shared_part = jnp.dot(shared_inner, shared_down, preferred_element_type=jnp.float32)
    both_parts = jnp.concatenate(
        [partial_out.reshape(slot_total, -1), shared_part], axis=0
    ).astype(jnp.bfloat16)
    both_columns = lax.psum_scatter(both_parts, "tp", scatter_dimension=1, tiled=True)
    expert_sums = both_columns[:slot_total]
    shared_sums = both_columns[slot_total:]
    results = expert_sums.reshape(per_owner, owner_count, slot_count, column_width).transpose(
        1, 0, 2, 3
    )
    shared_columns = shared_sums.astype(jnp.float32)
    returned = req_all_to_all(results)
    routed = jnp.dot(
        combine_matrix,
        returned.reshape(slot_total, column_width).astype(jnp.float32),
        precision=lax.Precision.HIGHEST,
    )
    next_hidden = (mixed_columns.astype(jnp.float32) + routed + shared_columns).astype(jnp.bfloat16)
    return (next_hidden, new_rows)


def solution(mesh):
    req = REQ_AXES
    in_specs = (
        P(req, "tp"),
        P(req),
        P(req, None),
        P(req, None),
        P(),
        P(None, "tp"),
        P(None, "tp"),
        P(),
        P("tp", None, None),
        P("tp", None, None),
        P("tp", None),
        P(),
        P(),
        P(req, None, "tp"),
        P(req, None, "tp"),
        P(req, "tp", None),
        P(None, "tp"),
        P(None, "tp"),
        P("tp", None),
    )
    out_specs = (P(req, "tp"), P(req, None))
    return jax.shard_map(
        shards, mesh=split_mesh(mesh), in_specs=in_specs, out_specs=out_specs, check_vma=False
    )
```

```python
import jax
import jax.numpy as jnp
from jax import lax
from jax.sharding import PartitionSpec as P

rope_base = 50000.0
route_scale = 2.446
norm_eps = 1e-06


def rms_norm(values, gains):
    widened = values.astype(jnp.float32)
    factor = lax.rsqrt(jnp.mean(widened * widened, axis=-1, keepdims=True) + norm_eps)
    return widened * factor * gains.astype(jnp.float32)


def rotate(values, positions):
    half_width = values.shape[-1] // 2
    exponent = jnp.arange(half_width, dtype=jnp.float32) * (2.0 / values.shape[-1])
    angles = positions[..., None] * jnp.power(rope_base, -exponent)
    cosine = jnp.cos(angles)
    sine_part = jnp.sin(angles)
    first_half = values[..., :half_width]
    second_half = values[..., half_width:]
    return jnp.concatenate(
        [
            first_half * cosine - second_half * sine_part,
            first_half * sine_part + second_half * cosine,
        ],
        axis=-1,
    )


def attend(queries, cache_rows, lengths, new_rows, score_scale, latent_width):
    starts = jnp.cumsum(lengths) - lengths
    places = jnp.arange(cache_rows.shape[0], dtype=jnp.int32)
    inside = (places[None, :] >= starts[:, None]) & (places[None, :] < (starts + lengths)[:, None])
    scores = (
        jnp.einsum("rhk,jk->rhj", queries, cache_rows, preferred_element_type=jnp.float32)
        * score_scale
    )
    own_score = (
        jnp.einsum("rhk,rk->rh", queries, new_rows, preferred_element_type=jnp.float32)
        * score_scale
    )
    highest = jnp.maximum(
        jnp.max(jnp.where(inside[:, None, :], scores, -jnp.inf), axis=-1), own_score
    )
    weights = jnp.where(inside[:, None, :], jnp.exp(scores - highest[..., None]), 0.0)
    own_weight = jnp.exp(own_score - highest)
    totals = jnp.sum(weights, axis=-1) + own_weight
    probabilities = (weights / totals[..., None]).astype(jnp.bfloat16)
    own_prob = (own_weight / totals).astype(jnp.bfloat16)
    summed = jnp.einsum(
        "rhj,jl->rhl",
        probabilities,
        cache_rows[:, :latent_width],
        preferred_element_type=jnp.float32,
    )
    summed = summed + own_prob.astype(jnp.float32)[..., None] * new_rows[
        :, None, :latent_width
    ].astype(jnp.float32)
    return summed.astype(jnp.bfloat16)


def gather_columns(values):
    parts = lax.axis_size("tp")
    copies = jnp.broadcast_to(values[None], (parts,) + values.shape)
    received = lax.all_to_all(copies, "tp", split_axis=0, concat_axis=0, tiled=True)
    return jnp.concatenate(list(received), axis=-1)


def shards(
    hidden,
    lengths,
    routes,
    latent_cache,
    attention_gain,
    query_weight,
    latent_weight,
    latent_gain,
    key_absorb,
    value_absorb,
    output_weight,
    feedforward_gain,
    router_weight,
    expert_gate,
    expert_up,
    expert_down,
    shared_gate,
    shared_up,
    shared_down,
):
    token_count = hidden.shape[0]
    owner_count = lax.axis_size("req")
    column_width = hidden.shape[1]
    column_start = lax.axis_index("tp") * column_width
    heads_here = key_absorb.shape[0]
    nope_width = key_absorb.shape[1]
    latent_width = key_absorb.shape[2]
    whole = gather_columns(hidden)
    normed = rms_norm(whole, attention_gain).astype(jnp.bfloat16)
    projected = jnp.dot(normed, query_weight, preferred_element_type=jnp.float32).reshape(
        token_count, heads_here, -1
    )
    rope_width = projected.shape[2] - nope_width
    positions = lengths.astype(jnp.float32)
    query_nope = projected[..., :nope_width].astype(jnp.bfloat16)
    query_rope = rotate(projected[..., nope_width:], positions[:, None]).astype(jnp.bfloat16)
    query_latent = jnp.einsum(
        "thn,hnl->thl", query_nope, key_absorb, preferred_element_type=jnp.float32
    ).astype(jnp.bfloat16)
    latent_part = jnp.dot(normed, latent_weight, preferred_element_type=jnp.float32).astype(
        jnp.bfloat16
    )
    latent_raw = gather_columns(latent_part)
    latent_new = rms_norm(latent_raw[:, :latent_width], latent_gain)
    key_new = rotate(latent_raw[:, latent_width:].astype(jnp.float32), positions)
    new_rows = jnp.concatenate([latent_new, key_new], axis=-1).astype(jnp.bfloat16)
    queries = jnp.concatenate([query_latent, query_rope], axis=-1)
    attended = attend(
        queries, latent_cache, lengths, new_rows, (nope_width + rope_width) ** (-0.5), latent_width
    )
    head_values = jnp.einsum(
        "thl,hlv->thv", attended, value_absorb, preferred_element_type=jnp.float32
    ).astype(jnp.bfloat16)
    attention = jnp.dot(
        head_values.reshape(token_count, -1), output_weight, preferred_element_type=jnp.float32
    )
    tp_count = lax.axis_size("tp")
    attention_blocks = attention.reshape(token_count, tp_count, column_width).transpose(1, 0, 2)
    attention_blocks = lax.all_to_all(attention_blocks, "tp", split_axis=0, concat_axis=0, tiled=True)
    attention_columns = jnp.sum(attention_blocks, axis=0)
    mixed_columns = (hidden.astype(jnp.float32) + attention_columns).astype(jnp.bfloat16)
    mixed = gather_columns(mixed_columns)
    expert_in = rms_norm(mixed, feedforward_gain).astype(jnp.bfloat16)
    logits = jnp.dot(expert_in, router_weight, preferred_element_type=jnp.float32)
    expert_count = router_weight.shape[1]
    top_count = routes.shape[1]
    per_owner = expert_count // owner_count
    slot_count = max(2, 8 * token_count * top_count // (3 * expert_count))
    chosen = jnp.take_along_axis(jax.nn.sigmoid(logits), routes, axis=1)
    route_weights = chosen / jnp.sum(chosen, axis=1, keepdims=True) * route_scale
    expert_ids = routes.reshape(-1)
    onehot = (expert_ids[:, None] == jnp.arange(expert_count, dtype=jnp.int32)[None, :]).astype(
        jnp.int32
    )
    earlier = jnp.cumsum(onehot, axis=0) - onehot
    slot_index = jnp.sum(earlier * onehot, axis=1)
    slot_places = (expert_ids * slot_count + slot_index).reshape(token_count, top_count)
    slot_total = expert_count * slot_count
    placed = slot_places[None, :, :] == jnp.arange(slot_total, dtype=jnp.int32)[:, None, None]
    gather_matrix = jnp.any(placed, axis=2).astype(jnp.bfloat16)
    combine_matrix = jnp.sum(jnp.where(placed, route_weights[None, :, :], 0.0), axis=2).T
    expert_columns = lax.dynamic_slice_in_dim(expert_in, column_start, column_width, 1)
    outgoing = jnp.dot(gather_matrix, expert_columns, preferred_element_type=jnp.float32).astype(
        jnp.bfloat16
    )
    outgoing = outgoing.reshape(owner_count, per_owner, slot_count, column_width)
    slab_columns = lax.all_to_all(outgoing, "req", split_axis=0, concat_axis=0, tiled=True)
    slab = lax.all_gather(slab_columns, "tp", axis=0, tiled=False)
    gate_blocks = expert_gate.reshape(per_owner, tp_count, column_width, -1)
    up_blocks = expert_up.reshape(per_owner, tp_count, column_width, -1)
    gate_part = jnp.einsum(
        "toesc,etcf->eosf", slab, gate_blocks, preferred_element_type=jnp.float32
    )
    up_part = jnp.einsum("toesc,etcf->eosf", slab, up_blocks, preferred_element_type=jnp.float32)
    inner_units = (jax.nn.silu(gate_part) * up_part).astype(jnp.bfloat16)
    partial_out = jnp.einsum(
        "eosf,efd->eosd", inner_units, expert_down, preferred_element_type=jnp.float32
    )
    shared_inner = (
        jax.nn.silu(jnp.dot(expert_in, shared_gate, preferred_element_type=jnp.float32))
        * jnp.dot(expert_in, shared_up, preferred_element_type=jnp.float32)
    ).astype(jnp.bfloat16)
    shared_part = jnp.dot(shared_inner, shared_down, preferred_element_type=jnp.float32)
    both_parts = jnp.concatenate(
        [partial_out.reshape(slot_total, -1), shared_part], axis=0
    ).astype(jnp.bfloat16)
    both_columns = lax.psum_scatter(both_parts, "tp", scatter_dimension=1, tiled=True)
    expert_sums = both_columns[:slot_total]
    shared_sums = both_columns[slot_total:]
    results = expert_sums.reshape(per_owner, owner_count, slot_count, column_width).transpose(
        1, 0, 2, 3
    )
    shared_columns = shared_sums.astype(jnp.float32)
    returned = lax.all_to_all(results, "req", split_axis=0, concat_axis=0, tiled=True)
    routed = jnp.dot(
        combine_matrix,
        returned.reshape(slot_total, column_width).astype(jnp.float32),
        precision=lax.Precision.HIGHEST,
    )
    next_hidden = (mixed_columns.astype(jnp.float32) + routed + shared_columns).astype(jnp.bfloat16)
    return (next_hidden, new_rows)


def solution(mesh):
    in_specs = (
        P("req", "tp"),
        P("req"),
        P("req", None),
        P("req", None),
        P(),
        P(None, "tp"),
        P(None, "tp"),
        P(),
        P("tp", None, None),
        P("tp", None, None),
        P("tp", None),
        P(),
        P(),
        P("req", None, "tp"),
        P("req", None, "tp"),
        P("req", "tp", None),
        P(None, "tp"),
        P(None, "tp"),
        P("tp", None),
    )
    out_specs = (P("req", "tp"), P("req", None))
    return jax.shard_map(shards, mesh=mesh, in_specs=in_specs, out_specs=out_specs, check_vma=False)
```

```python
import jax
import jax.numpy as jnp
from jax import lax
from jax.sharding import PartitionSpec as P

rope_base = 50000.0
route_scale = 2.446
norm_eps = 1e-06


def rms_norm(values, gains):
    widened = values.astype(jnp.float32)
    factor = lax.rsqrt(jnp.mean(widened * widened, axis=-1, keepdims=True) + norm_eps)
    return widened * factor * gains.astype(jnp.float32)


def rotate(values, positions):
    half_width = values.shape[-1] // 2
    exponent = jnp.arange(half_width, dtype=jnp.float32) * (2.0 / values.shape[-1])
    angles = positions[..., None] * jnp.power(rope_base, -exponent)
    cosine = jnp.cos(angles)
    sine_part = jnp.sin(angles)
    first_half = values[..., :half_width]
    second_half = values[..., half_width:]
    return jnp.concatenate(
        [
            first_half * cosine - second_half * sine_part,
            first_half * sine_part + second_half * cosine,
        ],
        axis=-1,
    )


def attend(queries, cache_rows, lengths, new_rows, score_scale, latent_width):
    starts = jnp.cumsum(lengths) - lengths
    places = jnp.arange(cache_rows.shape[0], dtype=jnp.int32)
    inside = (places[None, :] >= starts[:, None]) & (places[None, :] < (starts + lengths)[:, None])
    scores = (
        jnp.einsum("rhk,jk->rhj", queries, cache_rows, preferred_element_type=jnp.float32)
        * score_scale
    )
    own_score = (
        jnp.einsum("rhk,rk->rh", queries, new_rows, preferred_element_type=jnp.float32)
        * score_scale
    )
    highest = jnp.maximum(
        jnp.max(jnp.where(inside[:, None, :], scores, -jnp.inf), axis=-1), own_score
    )
    weights = jnp.where(inside[:, None, :], jnp.exp(scores - highest[..., None]), 0.0)
    own_weight = jnp.exp(own_score - highest)
    totals = jnp.sum(weights, axis=-1) + own_weight
    probabilities = (weights / totals[..., None]).astype(jnp.bfloat16)
    own_prob = (own_weight / totals).astype(jnp.bfloat16)
    summed = jnp.einsum(
        "rhj,jl->rhl",
        probabilities,
        cache_rows[:, :latent_width],
        preferred_element_type=jnp.float32,
    )
    summed = summed + own_prob.astype(jnp.float32)[..., None] * new_rows[
        :, None, :latent_width
    ].astype(jnp.float32)
    return summed.astype(jnp.bfloat16)


def shards(
    hidden,
    lengths,
    routes,
    latent_cache,
    attention_gain,
    query_weight,
    latent_weight,
    latent_gain,
    key_absorb,
    value_absorb,
    output_weight,
    feedforward_gain,
    router_weight,
    expert_gate,
    expert_up,
    expert_down,
    shared_gate,
    shared_up,
    shared_down,
):
    token_count = hidden.shape[0]
    owner_count = lax.axis_size("req")
    column_width = hidden.shape[1]
    column_start = lax.axis_index("tp") * column_width
    heads_here = key_absorb.shape[0]
    nope_width = key_absorb.shape[1]
    latent_width = key_absorb.shape[2]
    whole = lax.all_gather(hidden, "tp", axis=1, tiled=True)
    normed = rms_norm(whole, attention_gain).astype(jnp.bfloat16)
    projected = jnp.dot(normed, query_weight, preferred_element_type=jnp.float32).reshape(
        token_count, heads_here, -1
    )
    rope_width = projected.shape[2] - nope_width
    positions = lengths.astype(jnp.float32)
    query_nope = projected[..., :nope_width].astype(jnp.bfloat16)
    query_rope = rotate(projected[..., nope_width:], positions[:, None]).astype(jnp.bfloat16)
    query_latent = jnp.einsum(
        "thn,hnl->thl", query_nope, key_absorb, preferred_element_type=jnp.float32
    ).astype(jnp.bfloat16)
    latent_part = jnp.dot(normed, latent_weight, preferred_element_type=jnp.float32).astype(
        jnp.bfloat16
    )
    latent_raw = lax.all_gather(latent_part, "tp", axis=1, tiled=True)
    latent_new = rms_norm(latent_raw[:, :latent_width], latent_gain)
    key_new = rotate(latent_raw[:, latent_width:].astype(jnp.float32), positions)
    new_rows = jnp.concatenate([latent_new, key_new], axis=-1).astype(jnp.bfloat16)
    queries = jnp.concatenate([query_latent, query_rope], axis=-1)
    attended = attend(
        queries, latent_cache, lengths, new_rows, (nope_width + rope_width) ** (-0.5), latent_width
    )
    head_values = jnp.einsum(
        "thl,hlv->thv", attended, value_absorb, preferred_element_type=jnp.float32
    ).astype(jnp.bfloat16)
    attention = jnp.dot(
        head_values.reshape(token_count, -1), output_weight, preferred_element_type=jnp.float32
    )
    tp_count = lax.axis_size("tp")
    attention_blocks = attention.reshape(token_count, tp_count, column_width).transpose(1, 0, 2)
    attention_blocks = lax.all_to_all(attention_blocks, "tp", split_axis=0, concat_axis=0, tiled=True)
    attention_columns = jnp.sum(attention_blocks, axis=0)
    mixed_columns = (hidden.astype(jnp.float32) + attention_columns).astype(jnp.bfloat16)
    mixed = lax.all_gather(mixed_columns, "tp", axis=1, tiled=True)
    expert_in = rms_norm(mixed, feedforward_gain).astype(jnp.bfloat16)
    shared_inner = (
        jax.nn.silu(jnp.dot(expert_in, shared_gate, preferred_element_type=jnp.float32))
        * jnp.dot(expert_in, shared_up, preferred_element_type=jnp.float32)
    ).astype(jnp.bfloat16)
    shared_part = jnp.dot(shared_inner, shared_down, preferred_element_type=jnp.float32)
    shared_columns = lax.psum_scatter(shared_part, "tp", scatter_dimension=1, tiled=True)
    logits = jnp.dot(expert_in, router_weight, preferred_element_type=jnp.float32)
    expert_count = router_weight.shape[1]
    top_count = routes.shape[1]
    per_owner = expert_count // owner_count
    slot_count = max(2, 8 * token_count * top_count // (3 * expert_count))
    chosen = jnp.take_along_axis(jax.nn.sigmoid(logits), routes, axis=1)
    route_weights = chosen / jnp.sum(chosen, axis=1, keepdims=True) * route_scale
    expert_ids = routes.reshape(-1)
    onehot = (expert_ids[:, None] == jnp.arange(expert_count, dtype=jnp.int32)[None, :]).astype(
        jnp.int32
    )
    earlier = jnp.cumsum(onehot, axis=0) - onehot
    slot_index = jnp.sum(earlier * onehot, axis=1)
    slot_places = (expert_ids * slot_count + slot_index).reshape(token_count, top_count)
    slot_total = expert_count * slot_count
    placed = slot_places[None, :, :] == jnp.arange(slot_total, dtype=jnp.int32)[:, None, None]
    gather_matrix = jnp.any(placed, axis=2).astype(jnp.bfloat16)
    combine_matrix = jnp.sum(jnp.where(placed, route_weights[None, :, :], 0.0), axis=2).T
    expert_columns = lax.dynamic_slice_in_dim(expert_in, column_start, column_width, 1)
    outgoing = jnp.dot(gather_matrix, expert_columns, preferred_element_type=jnp.float32).astype(
        jnp.bfloat16
    )
    outgoing = outgoing.reshape(owner_count, per_owner, slot_count, column_width)
    slab_columns = lax.all_to_all(outgoing, "req", split_axis=0, concat_axis=0, tiled=True)
    slab = lax.all_gather(slab_columns, "tp", axis=0, tiled=False)
    gate_blocks = expert_gate.reshape(per_owner, tp_count, column_width, -1)
    up_blocks = expert_up.reshape(per_owner, tp_count, column_width, -1)
    gate_part = jnp.einsum(
        "toesc,etcf->eosf", slab, gate_blocks, preferred_element_type=jnp.float32
    )
    up_part = jnp.einsum("toesc,etcf->eosf", slab, up_blocks, preferred_element_type=jnp.float32)
    inner_units = (jax.nn.silu(gate_part) * up_part).astype(jnp.bfloat16)
    partial_out = jnp.einsum(
        "eosf,efd->eosd", inner_units, expert_down, preferred_element_type=jnp.float32
    )
    expert_sums = lax.psum_scatter(
        partial_out.reshape(slot_total, -1).astype(jnp.bfloat16),
        "tp",
        scatter_dimension=1,
        tiled=True,
    )
    results = expert_sums.reshape(per_owner, owner_count, slot_count, column_width).transpose(
        1, 0, 2, 3
    )
    returned = lax.all_to_all(results, "req", split_axis=0, concat_axis=0, tiled=True)
    routed = jnp.dot(
        combine_matrix,
        returned.reshape(slot_total, column_width).astype(jnp.float32),
        precision=lax.Precision.HIGHEST,
    )
    next_hidden = (mixed_columns.astype(jnp.float32) + routed + shared_columns).astype(jnp.bfloat16)
    return (next_hidden, new_rows)


def solution(mesh):
    in_specs = (
        P("req", "tp"),
        P("req"),
        P("req", None),
        P("req", None),
        P(),
        P(None, "tp"),
        P(None, "tp"),
        P(),
        P("tp", None, None),
        P("tp", None, None),
        P("tp", None),
        P(),
        P(),
        P("req", None, "tp"),
        P("req", None, "tp"),
        P("req", "tp", None),
        P(None, "tp"),
        P(None, "tp"),
        P("tp", None),
    )
    out_specs = (P("req", "tp"), P("req", None))
    return jax.shard_map(shards, mesh=mesh, in_specs=in_specs, out_specs=out_specs, check_vma=False)
```

```python
import jax
import jax.numpy as jnp
from jax import lax
from jax.sharding import PartitionSpec as P

rope_base = 50000.0
route_scale = 2.446
norm_eps = 1e-06


def rms_norm(values, gains):
    widened = values.astype(jnp.float32)
    factor = lax.rsqrt(jnp.mean(widened * widened, axis=-1, keepdims=True) + norm_eps)
    return widened * factor * gains.astype(jnp.float32)


def rotate(values, positions):
    half_width = values.shape[-1] // 2
    exponent = jnp.arange(half_width, dtype=jnp.float32) * (2.0 / values.shape[-1])
    angles = positions[..., None] * jnp.power(rope_base, -exponent)
    cosine = jnp.cos(angles)
    sine_part = jnp.sin(angles)
    first_half = values[..., :half_width]
    second_half = values[..., half_width:]
    return jnp.concatenate(
        [
            first_half * cosine - second_half * sine_part,
            first_half * sine_part + second_half * cosine,
        ],
        axis=-1,
    )


def attend(queries, cache_rows, lengths, new_rows, score_scale, latent_width):
    starts = jnp.cumsum(lengths) - lengths
    places = jnp.arange(cache_rows.shape[0], dtype=jnp.int32)
    inside = (places[None, :] >= starts[:, None]) & (places[None, :] < (starts + lengths)[:, None])
    scores = (
        jnp.einsum("rhk,jk->rhj", queries, cache_rows, preferred_element_type=jnp.float32)
        * score_scale
    )
    own_score = (
        jnp.einsum("rhk,rk->rh", queries, new_rows, preferred_element_type=jnp.float32)
        * score_scale
    )
    highest = jnp.maximum(
        jnp.max(jnp.where(inside[:, None, :], scores, -jnp.inf), axis=-1), own_score
    )
    weights = jnp.where(inside[:, None, :], jnp.exp(scores - highest[..., None]), 0.0)
    own_weight = jnp.exp(own_score - highest)
    totals = jnp.sum(weights, axis=-1) + own_weight
    probabilities = (weights / totals[..., None]).astype(jnp.bfloat16)
    own_prob = (own_weight / totals).astype(jnp.bfloat16)
    summed = jnp.einsum(
        "rhj,jl->rhl",
        probabilities,
        cache_rows[:, :latent_width],
        preferred_element_type=jnp.float32,
    )
    summed = summed + own_prob.astype(jnp.float32)[..., None] * new_rows[
        :, None, :latent_width
    ].astype(jnp.float32)
    return summed.astype(jnp.bfloat16)


def shards(
    hidden,
    lengths,
    routes,
    latent_cache,
    attention_gain,
    query_weight,
    latent_weight,
    latent_gain,
    key_absorb,
    value_absorb,
    output_weight,
    feedforward_gain,
    router_weight,
    expert_gate,
    expert_up,
    expert_down,
    shared_gate,
    shared_up,
    shared_down,
):
    token_count = hidden.shape[0]
    owner_count = lax.axis_size("req")
    column_width = hidden.shape[1]
    column_start = lax.axis_index("tp") * column_width
    heads_here = key_absorb.shape[0]
    nope_width = key_absorb.shape[1]
    latent_width = key_absorb.shape[2]
    whole = lax.all_gather(hidden, "tp", axis=1, tiled=True)
    normed = rms_norm(whole, attention_gain).astype(jnp.bfloat16)
    projected = jnp.dot(normed, query_weight, preferred_element_type=jnp.float32).reshape(
        token_count, heads_here, -1
    )
    rope_width = projected.shape[2] - nope_width
    positions = lengths.astype(jnp.float32)
    query_nope = projected[..., :nope_width].astype(jnp.bfloat16)
    query_rope = rotate(projected[..., nope_width:], positions[:, None]).astype(jnp.bfloat16)
    query_latent = jnp.einsum(
        "thn,hnl->thl", query_nope, key_absorb, preferred_element_type=jnp.float32
    ).astype(jnp.bfloat16)
    latent_part = jnp.dot(normed, latent_weight, preferred_element_type=jnp.float32).astype(
        jnp.bfloat16
    )
    latent_raw = lax.all_gather(latent_part, "tp", axis=1, tiled=True)
    latent_new = rms_norm(latent_raw[:, :latent_width], latent_gain)
    key_new = rotate(latent_raw[:, latent_width:].astype(jnp.float32), positions)
    new_rows = jnp.concatenate([latent_new, key_new], axis=-1).astype(jnp.bfloat16)
    queries = jnp.concatenate([query_latent, query_rope], axis=-1)
    attended = attend(
        queries, latent_cache, lengths, new_rows, (nope_width + rope_width) ** (-0.5), latent_width
    )
    head_values = jnp.einsum(
        "thl,hlv->thv", attended, value_absorb, preferred_element_type=jnp.float32
    ).astype(jnp.bfloat16)
    attention = jnp.dot(
        head_values.reshape(token_count, -1), output_weight, preferred_element_type=jnp.float32
    )
    tp_count = lax.axis_size("tp")
    attention_blocks = attention.reshape(token_count, tp_count, column_width).transpose(1, 0, 2)
    attention_blocks = lax.all_to_all(attention_blocks, "tp", split_axis=0, concat_axis=0, tiled=True)
    attention_columns = jnp.sum(attention_blocks, axis=0)
    mixed_columns = (hidden.astype(jnp.float32) + attention_columns).astype(jnp.bfloat16)
    mixed = lax.all_gather(mixed_columns, "tp", axis=1, tiled=True)
    expert_in = rms_norm(mixed, feedforward_gain).astype(jnp.bfloat16)
    shared_inner = (
        jax.nn.silu(jnp.dot(expert_in, shared_gate, preferred_element_type=jnp.float32))
        * jnp.dot(expert_in, shared_up, preferred_element_type=jnp.float32)
    ).astype(jnp.bfloat16)
    shared_part = jnp.dot(shared_inner, shared_down, preferred_element_type=jnp.float32)
    shared_columns = lax.psum_scatter(shared_part, "tp", scatter_dimension=1, tiled=True)
    logits = jnp.dot(expert_in, router_weight, preferred_element_type=jnp.float32)
    expert_count = router_weight.shape[1]
    top_count = routes.shape[1]
    per_owner = expert_count // owner_count
    slot_count = max(2, 8 * token_count * top_count // (3 * expert_count))
    chosen = jnp.take_along_axis(jax.nn.sigmoid(logits), routes, axis=1)
    route_weights = chosen / jnp.sum(chosen, axis=1, keepdims=True) * route_scale
    expert_ids = routes.reshape(-1)
    onehot = (expert_ids[:, None] == jnp.arange(expert_count, dtype=jnp.int32)[None, :]).astype(
        jnp.int32
    )
    earlier = jnp.cumsum(onehot, axis=0) - onehot
    slot_index = jnp.sum(earlier * onehot, axis=1)
    slot_places = (expert_ids * slot_count + slot_index).reshape(token_count, top_count)
    slot_total = expert_count * slot_count
    placed = slot_places[None, :, :] == jnp.arange(slot_total, dtype=jnp.int32)[:, None, None]
    gather_matrix = jnp.any(placed, axis=2).astype(jnp.bfloat16)
    combine_matrix = jnp.sum(jnp.where(placed, route_weights[None, :, :], 0.0), axis=2).T
    expert_columns = lax.dynamic_slice_in_dim(expert_in, column_start, column_width, 1)
    outgoing = jnp.dot(gather_matrix, expert_columns, preferred_element_type=jnp.float32).astype(
        jnp.bfloat16
    )
    outgoing = outgoing.reshape(owner_count, per_owner, slot_count, column_width)
    slab_columns = lax.all_to_all(outgoing, "req", split_axis=0, concat_axis=0, tiled=True)
    slab_columns, shared_columns = lax.optimization_barrier((slab_columns, shared_columns))
    slab = lax.all_gather(slab_columns, "tp", axis=0, tiled=False)
    gate_blocks = expert_gate.reshape(per_owner, tp_count, column_width, -1)
    up_blocks = expert_up.reshape(per_owner, tp_count, column_width, -1)
    gate_part = jnp.einsum(
        "toesc,etcf->eosf", slab, gate_blocks, preferred_element_type=jnp.float32
    )
    up_part = jnp.einsum("toesc,etcf->eosf", slab, up_blocks, preferred_element_type=jnp.float32)
    inner_units = (jax.nn.silu(gate_part) * up_part).astype(jnp.bfloat16)
    partial_out = jnp.einsum(
        "eosf,efd->eosd", inner_units, expert_down, preferred_element_type=jnp.float32
    )
    expert_sums = lax.psum_scatter(
        partial_out.reshape(slot_total, -1).astype(jnp.bfloat16),
        "tp",
        scatter_dimension=1,
        tiled=True,
    )
    results = expert_sums.reshape(per_owner, owner_count, slot_count, column_width).transpose(
        1, 0, 2, 3
    )
    returned = lax.all_to_all(results, "req", split_axis=0, concat_axis=0, tiled=True)
    routed = jnp.dot(
        combine_matrix,
        returned.reshape(slot_total, column_width).astype(jnp.float32),
        precision=lax.Precision.HIGHEST,
    )
    next_hidden = (mixed_columns.astype(jnp.float32) + routed + shared_columns).astype(jnp.bfloat16)
    return (next_hidden, new_rows)


def solution(mesh):
    in_specs = (
        P("req", "tp"),
        P("req"),
        P("req", None),
        P("req", None),
        P(),
        P(None, "tp"),
        P(None, "tp"),
        P(),
        P("tp", None, None),
        P("tp", None, None),
        P("tp", None),
        P(),
        P(),
        P("req", None, "tp"),
        P("req", None, "tp"),
        P("req", "tp", None),
        P(None, "tp"),
        P(None, "tp"),
        P("tp", None),
    )
    out_specs = (P("req", "tp"), P("req", None))
    return jax.shard_map(shards, mesh=mesh, in_specs=in_specs, out_specs=out_specs, check_vma=False)
```

```python
import jax
import jax.numpy as jnp
from jax import lax
from jax.sharding import PartitionSpec as P

rope_base = 50000.0
route_scale = 2.446
norm_eps = 1e-06


def rms_norm(values, gains):
    widened = values.astype(jnp.float32)
    factor = lax.rsqrt(jnp.mean(widened * widened, axis=-1, keepdims=True) + norm_eps)
    return widened * factor * gains.astype(jnp.float32)


def rotate(values, positions):
    half_width = values.shape[-1] // 2
    exponent = jnp.arange(half_width, dtype=jnp.float32) * (2.0 / values.shape[-1])
    angles = positions[..., None] * jnp.power(rope_base, -exponent)
    cosine = jnp.cos(angles)
    sine_part = jnp.sin(angles)
    first_half = values[..., :half_width]
    second_half = values[..., half_width:]
    return jnp.concatenate(
        [
            first_half * cosine - second_half * sine_part,
            first_half * sine_part + second_half * cosine,
        ],
        axis=-1,
    )


def attend(queries, cache_rows, lengths, new_rows, score_scale, latent_width):
    starts = jnp.cumsum(lengths) - lengths
    places = jnp.arange(cache_rows.shape[0], dtype=jnp.int32)
    inside = (places[None, :] >= starts[:, None]) & (places[None, :] < (starts + lengths)[:, None])
    scores = (
        jnp.einsum("rhk,jk->rhj", queries, cache_rows, preferred_element_type=jnp.float32)
        * score_scale
    )
    own_score = (
        jnp.einsum("rhk,rk->rh", queries, new_rows, preferred_element_type=jnp.float32)
        * score_scale
    )
    highest = jnp.maximum(
        jnp.max(jnp.where(inside[:, None, :], scores, -jnp.inf), axis=-1), own_score
    )
    weights = jnp.where(inside[:, None, :], jnp.exp(scores - highest[..., None]), 0.0)
    own_weight = jnp.exp(own_score - highest)
    totals = jnp.sum(weights, axis=-1) + own_weight
    probabilities = (weights / totals[..., None]).astype(jnp.bfloat16)
    own_prob = (own_weight / totals).astype(jnp.bfloat16)
    summed = jnp.einsum(
        "rhj,jl->rhl",
        probabilities,
        cache_rows[:, :latent_width],
        preferred_element_type=jnp.float32,
    )
    summed = summed + own_prob.astype(jnp.float32)[..., None] * new_rows[
        :, None, :latent_width
    ].astype(jnp.float32)
    return summed.astype(jnp.bfloat16)


def shards(
    hidden,
    lengths,
    routes,
    latent_cache,
    attention_gain,
    query_weight,
    latent_weight,
    latent_gain,
    key_absorb,
    value_absorb,
    output_weight,
    feedforward_gain,
    router_weight,
    expert_gate,
    expert_up,
    expert_down,
    shared_gate,
    shared_up,
    shared_down,
):
    token_count = hidden.shape[0]
    owner_count = lax.axis_size("req")
    column_width = hidden.shape[1]
    column_start = lax.axis_index("tp") * column_width
    heads_here = key_absorb.shape[0]
    nope_width = key_absorb.shape[1]
    latent_width = key_absorb.shape[2]
    whole = lax.all_gather(hidden, "tp", axis=1, tiled=True)
    normed = rms_norm(whole, attention_gain).astype(jnp.bfloat16)
    projected = jnp.dot(normed, query_weight, preferred_element_type=jnp.float32).reshape(
        token_count, heads_here, -1
    )
    rope_width = projected.shape[2] - nope_width
    positions = lengths.astype(jnp.float32)
    query_nope = projected[..., :nope_width].astype(jnp.bfloat16)
    query_rope = rotate(projected[..., nope_width:], positions[:, None]).astype(jnp.bfloat16)
    query_latent = jnp.einsum(
        "thn,hnl->thl", query_nope, key_absorb, preferred_element_type=jnp.float32
    ).astype(jnp.bfloat16)
    latent_full = lax.all_gather(latent_weight, "tp", axis=1, tiled=True)
    latent_raw = jnp.dot(normed, latent_full, preferred_element_type=jnp.float32).astype(
        jnp.bfloat16
    )
    latent_new = rms_norm(latent_raw[:, :latent_width], latent_gain)
    key_new = rotate(latent_raw[:, latent_width:].astype(jnp.float32), positions)
    new_rows = jnp.concatenate([latent_new, key_new], axis=-1).astype(jnp.bfloat16)
    queries = jnp.concatenate([query_latent, query_rope], axis=-1)
    attended = attend(
        queries, latent_cache, lengths, new_rows, (nope_width + rope_width) ** (-0.5), latent_width
    )
    head_values = jnp.einsum(
        "thl,hlv->thv", attended, value_absorb, preferred_element_type=jnp.float32
    ).astype(jnp.bfloat16)
    attention = jnp.dot(
        head_values.reshape(token_count, -1), output_weight, preferred_element_type=jnp.float32
    )
    tp_count = lax.axis_size("tp")
    attention_blocks = attention.reshape(token_count, tp_count, column_width).transpose(1, 0, 2)
    attention_blocks = lax.all_to_all(attention_blocks, "tp", split_axis=0, concat_axis=0, tiled=True)
    attention_columns = jnp.sum(attention_blocks, axis=0)
    mixed_columns = (hidden.astype(jnp.float32) + attention_columns).astype(jnp.bfloat16)
    mixed = lax.all_gather(mixed_columns, "tp", axis=1, tiled=True)
    expert_in = rms_norm(mixed, feedforward_gain).astype(jnp.bfloat16)
    logits = jnp.dot(expert_in, router_weight, preferred_element_type=jnp.float32)
    expert_count = router_weight.shape[1]
    top_count = routes.shape[1]
    per_owner = expert_count // owner_count
    slot_count = max(2, 8 * token_count * top_count // (3 * expert_count))
    chosen = jnp.take_along_axis(jax.nn.sigmoid(logits), routes, axis=1)
    route_weights = chosen / jnp.sum(chosen, axis=1, keepdims=True) * route_scale
    expert_ids = routes.reshape(-1)
    onehot = (expert_ids[:, None] == jnp.arange(expert_count, dtype=jnp.int32)[None, :]).astype(
        jnp.int32
    )
    earlier = jnp.cumsum(onehot, axis=0) - onehot
    slot_index = jnp.sum(earlier * onehot, axis=1)
    slot_places = (expert_ids * slot_count + slot_index).reshape(token_count, top_count)
    slot_total = expert_count * slot_count
    placed = slot_places[None, :, :] == jnp.arange(slot_total, dtype=jnp.int32)[:, None, None]
    gather_matrix = jnp.any(placed, axis=2).astype(jnp.bfloat16)
    combine_matrix = jnp.sum(jnp.where(placed, route_weights[None, :, :], 0.0), axis=2).T
    expert_columns = lax.dynamic_slice_in_dim(expert_in, column_start, column_width, 1)
    outgoing = jnp.dot(gather_matrix, expert_columns, preferred_element_type=jnp.float32).astype(
        jnp.bfloat16
    )
    outgoing = outgoing.reshape(owner_count, per_owner, slot_count, column_width)
    slab_columns = lax.all_to_all(outgoing, "req", split_axis=0, concat_axis=0, tiled=True)
    slab = lax.all_gather(slab_columns, "tp", axis=0, tiled=False)
    gate_blocks = expert_gate.reshape(per_owner, tp_count, column_width, -1)
    up_blocks = expert_up.reshape(per_owner, tp_count, column_width, -1)
    gate_part = jnp.einsum(
        "toesc,etcf->eosf", slab, gate_blocks, preferred_element_type=jnp.float32
    )
    up_part = jnp.einsum("toesc,etcf->eosf", slab, up_blocks, preferred_element_type=jnp.float32)
    inner_units = (jax.nn.silu(gate_part) * up_part).astype(jnp.bfloat16)
    partial_out = jnp.einsum(
        "eosf,efd->eosd", inner_units, expert_down, preferred_element_type=jnp.float32
    )
    shared_inner = (
        jax.nn.silu(jnp.dot(expert_in, shared_gate, preferred_element_type=jnp.float32))
        * jnp.dot(expert_in, shared_up, preferred_element_type=jnp.float32)
    ).astype(jnp.bfloat16)
    shared_part = jnp.dot(shared_inner, shared_down, preferred_element_type=jnp.float32)
    both_parts = jnp.concatenate(
        [partial_out.reshape(slot_total, -1), shared_part], axis=0
    ).astype(jnp.bfloat16)
    both_columns = lax.psum_scatter(both_parts, "tp", scatter_dimension=1, tiled=True)
    expert_sums = both_columns[:slot_total]
    shared_sums = both_columns[slot_total:]
    results = expert_sums.reshape(per_owner, owner_count, slot_count, column_width).transpose(
        1, 0, 2, 3
    )
    shared_columns = shared_sums.astype(jnp.float32)
    returned = lax.all_to_all(results, "req", split_axis=0, concat_axis=0, tiled=True)
    routed = jnp.dot(
        combine_matrix,
        returned.reshape(slot_total, column_width).astype(jnp.float32),
        precision=lax.Precision.HIGHEST,
    )
    next_hidden = (mixed_columns.astype(jnp.float32) + routed + shared_columns).astype(jnp.bfloat16)
    return (next_hidden, new_rows)


def solution(mesh):
    in_specs = (
        P("req", "tp"),
        P("req"),
        P("req", None),
        P("req", None),
        P(),
        P(None, "tp"),
        P(None, "tp"),
        P(),
        P("tp", None, None),
        P("tp", None, None),
        P("tp", None),
        P(),
        P(),
        P("req", None, "tp"),
        P("req", None, "tp"),
        P("req", "tp", None),
        P(None, "tp"),
        P(None, "tp"),
        P("tp", None),
    )
    out_specs = (P("req", "tp"), P("req", None))
    return jax.shard_map(shards, mesh=mesh, in_specs=in_specs, out_specs=out_specs, check_vma=False)
```

```python
import jax
import jax.numpy as jnp
from jax import lax
from jax.sharding import PartitionSpec as P

rope_base = 50000.0
route_scale = 2.446
norm_eps = 1e-06


def rms_norm(values, gains):
    widened = values.astype(jnp.float32)
    factor = lax.rsqrt(jnp.mean(widened * widened, axis=-1, keepdims=True) + norm_eps)
    return widened * factor * gains.astype(jnp.float32)


def rotate(values, positions):
    half_width = values.shape[-1] // 2
    exponent = jnp.arange(half_width, dtype=jnp.float32) * (2.0 / values.shape[-1])
    angles = positions[..., None] * jnp.power(rope_base, -exponent)
    cosine = jnp.cos(angles)
    sine_part = jnp.sin(angles)
    first_half = values[..., :half_width]
    second_half = values[..., half_width:]
    return jnp.concatenate(
        [
            first_half * cosine - second_half * sine_part,
            first_half * sine_part + second_half * cosine,
        ],
        axis=-1,
    )


def attend(queries, cache_rows, lengths, new_rows, score_scale, latent_width):
    starts = jnp.cumsum(lengths) - lengths
    places = jnp.arange(cache_rows.shape[0], dtype=jnp.int32)
    inside = (places[None, :] >= starts[:, None]) & (places[None, :] < (starts + lengths)[:, None])
    scores = (
        jnp.einsum("rhk,jk->rhj", queries, cache_rows, preferred_element_type=jnp.float32)
        * score_scale
    )
    own_score = (
        jnp.einsum("rhk,rk->rh", queries, new_rows, preferred_element_type=jnp.float32)
        * score_scale
    )
    highest = jnp.maximum(
        jnp.max(jnp.where(inside[:, None, :], scores, -jnp.inf), axis=-1), own_score
    )
    weights = jnp.where(inside[:, None, :], jnp.exp(scores - highest[..., None]), 0.0)
    own_weight = jnp.exp(own_score - highest)
    totals = jnp.sum(weights, axis=-1) + own_weight
    probabilities = (weights / totals[..., None]).astype(jnp.bfloat16)
    own_prob = (own_weight / totals).astype(jnp.bfloat16)
    summed = jnp.einsum(
        "rhj,jl->rhl",
        probabilities,
        cache_rows[:, :latent_width],
        preferred_element_type=jnp.float32,
    )
    summed = summed + own_prob.astype(jnp.float32)[..., None] * new_rows[
        :, None, :latent_width
    ].astype(jnp.float32)
    return summed.astype(jnp.bfloat16)


def shards(
    hidden,
    lengths,
    routes,
    latent_cache,
    attention_gain,
    query_weight,
    latent_weight,
    latent_gain,
    key_absorb,
    value_absorb,
    output_weight,
    feedforward_gain,
    router_weight,
    expert_gate,
    expert_up,
    expert_down,
    shared_gate,
    shared_up,
    shared_down,
):
    token_count = hidden.shape[0]
    owner_count = lax.axis_size("req")
    column_width = hidden.shape[1]
    column_start = lax.axis_index("tp") * column_width
    heads_here = key_absorb.shape[0]
    nope_width = key_absorb.shape[1]
    latent_width = key_absorb.shape[2]
    whole = lax.all_gather(hidden, "tp", axis=1, tiled=True)
    normed = rms_norm(whole, attention_gain).astype(jnp.bfloat16)
    projected = jnp.dot(normed, query_weight, preferred_element_type=jnp.float32).reshape(
        token_count, heads_here, -1
    )
    rope_width = projected.shape[2] - nope_width
    positions = lengths.astype(jnp.float32)
    query_nope = projected[..., :nope_width].astype(jnp.bfloat16)
    query_rope = rotate(projected[..., nope_width:], positions[:, None]).astype(jnp.bfloat16)
    query_latent = jnp.einsum(
        "thn,hnl->thl", query_nope, key_absorb, preferred_element_type=jnp.float32
    ).astype(jnp.bfloat16)
    latent_part = jnp.dot(normed, latent_weight, preferred_element_type=jnp.float32).astype(
        jnp.bfloat16
    )
    latent_raw = lax.all_gather(latent_part, "tp", axis=1, tiled=True)
    latent_new = rms_norm(latent_raw[:, :latent_width], latent_gain)
    key_new = rotate(latent_raw[:, latent_width:].astype(jnp.float32), positions)
    new_rows = jnp.concatenate([latent_new, key_new], axis=-1).astype(jnp.bfloat16)
    queries = jnp.concatenate([query_latent, query_rope], axis=-1)
    attended = attend(
        queries, latent_cache, lengths, new_rows, (nope_width + rope_width) ** (-0.5), latent_width
    )
    head_values = jnp.einsum(
        "thl,hlv->thv", attended, value_absorb, preferred_element_type=jnp.float32
    ).astype(jnp.bfloat16)
    attention = jnp.dot(
        head_values.reshape(token_count, -1), output_weight, preferred_element_type=jnp.float32
    )
    tp_count = lax.axis_size("tp")
    attention_blocks = (
        attention.reshape(token_count, tp_count, column_width).transpose(1, 0, 2).astype(jnp.bfloat16)
    )
    attention_blocks = lax.all_to_all(attention_blocks, "tp", split_axis=0, concat_axis=0, tiled=True)
    attention_columns = jnp.sum(attention_blocks.astype(jnp.float32), axis=0)
    mixed_columns = (hidden.astype(jnp.float32) + attention_columns).astype(jnp.bfloat16)
    mixed = lax.all_gather(mixed_columns, "tp", axis=1, tiled=True)
    expert_in = rms_norm(mixed, feedforward_gain).astype(jnp.bfloat16)
    logits = jnp.dot(expert_in, router_weight, preferred_element_type=jnp.float32)
    expert_count = router_weight.shape[1]
    top_count = routes.shape[1]
    per_owner = expert_count // owner_count
    slot_count = max(2, 8 * token_count * top_count // (3 * expert_count))
    chosen = jnp.take_along_axis(jax.nn.sigmoid(logits), routes, axis=1)
    route_weights = chosen / jnp.sum(chosen, axis=1, keepdims=True) * route_scale
    expert_ids = routes.reshape(-1)
    onehot = (expert_ids[:, None] == jnp.arange(expert_count, dtype=jnp.int32)[None, :]).astype(
        jnp.int32
    )
    earlier = jnp.cumsum(onehot, axis=0) - onehot
    slot_index = jnp.sum(earlier * onehot, axis=1)
    slot_places = (expert_ids * slot_count + slot_index).reshape(token_count, top_count)
    slot_total = expert_count * slot_count
    placed = slot_places[None, :, :] == jnp.arange(slot_total, dtype=jnp.int32)[:, None, None]
    gather_matrix = jnp.any(placed, axis=2).astype(jnp.bfloat16)
    combine_matrix = jnp.sum(jnp.where(placed, route_weights[None, :, :], 0.0), axis=2).T
    expert_columns = lax.dynamic_slice_in_dim(expert_in, column_start, column_width, 1)
    outgoing = jnp.dot(gather_matrix, expert_columns, preferred_element_type=jnp.float32).astype(
        jnp.bfloat16
    )
    outgoing = outgoing.reshape(owner_count, per_owner, slot_count, column_width)
    slab_columns = lax.all_to_all(outgoing, "req", split_axis=0, concat_axis=0, tiled=True)
    slab = lax.all_gather(slab_columns, "tp", axis=0, tiled=False)
    gate_blocks = expert_gate.reshape(per_owner, tp_count, column_width, -1)
    up_blocks = expert_up.reshape(per_owner, tp_count, column_width, -1)
    gate_part = jnp.einsum(
        "toesc,etcf->eosf", slab, gate_blocks, preferred_element_type=jnp.float32
    )
    up_part = jnp.einsum("toesc,etcf->eosf", slab, up_blocks, preferred_element_type=jnp.float32)
    inner_units = (jax.nn.silu(gate_part) * up_part).astype(jnp.bfloat16)
    partial_out = jnp.einsum(
        "eosf,efd->eosd", inner_units, expert_down, preferred_element_type=jnp.float32
    )
    shared_inner = (
        jax.nn.silu(jnp.dot(expert_in, shared_gate, preferred_element_type=jnp.float32))
        * jnp.dot(expert_in, shared_up, preferred_element_type=jnp.float32)
    ).astype(jnp.bfloat16)
    shared_part = jnp.dot(shared_inner, shared_down, preferred_element_type=jnp.float32)
    both_parts = jnp.concatenate(
        [partial_out.reshape(slot_total, -1), shared_part], axis=0
    ).astype(jnp.bfloat16)
    both_columns = lax.psum_scatter(both_parts, "tp", scatter_dimension=1, tiled=True)
    expert_sums = both_columns[:slot_total]
    shared_sums = both_columns[slot_total:]
    results = expert_sums.reshape(per_owner, owner_count, slot_count, column_width).transpose(
        1, 0, 2, 3
    )
    shared_columns = shared_sums.astype(jnp.float32)
    returned = lax.all_to_all(results, "req", split_axis=0, concat_axis=0, tiled=True)
    routed = jnp.dot(
        combine_matrix,
        returned.reshape(slot_total, column_width).astype(jnp.float32),
        precision=lax.Precision.HIGHEST,
    )
    next_hidden = (mixed_columns.astype(jnp.float32) + routed + shared_columns).astype(jnp.bfloat16)
    return (next_hidden, new_rows)


def solution(mesh):
    in_specs = (
        P("req", "tp"),
        P("req"),
        P("req", None),
        P("req", None),
        P(),
        P(None, "tp"),
        P(None, "tp"),
        P(),
        P("tp", None, None),
        P("tp", None, None),
        P("tp", None),
        P(),
        P(),
        P("req", None, "tp"),
        P("req", None, "tp"),
        P("req", "tp", None),
        P(None, "tp"),
        P(None, "tp"),
        P("tp", None),
    )
    out_specs = (P("req", "tp"), P("req", None))
    return jax.shard_map(shards, mesh=mesh, in_specs=in_specs, out_specs=out_specs, check_vma=False)
```
